256 devices in a mesh: leaf: 2 (over core), row: 8 (over z), col: 16 (over y, x).
Axes of the slice: x: 4, y: 4, z: 8, core: 2. Of those that a mesh axis runs over, the one named last changes fastest.
Arguments:
- front: float32 [2, 8, 8, 128, 4, 16, 128], P('leaf', None, 'row', None, None, 'col'), as said below
- parent: float32 [4, 2, 8, 128, 4, 16, 128], P(None, 'leaf', 'row', None, None, 'col'), may hold values from -0.2 to 0.2
- tile_map: int32 [2, 56], replicated, may hold values from 0 to 63, as said below
- col_shift: int32 [4], replicated, may hold values from 0 to 7
Outputs:
- factored: float32 [2, 8, 8, 128, 4, 16, 128], P('leaf', None, 'row', None, None, 'col')
- new_parent: float32 [4, 2, 8, 128, 4, 16, 128], P(None, 'leaf', 'row', None, None, 'col')
The draws below stay inside these ranges and needn't reach their ends.
Inputs may be any that keep to these rules, and one draw needn't show every extreme that they name: For each leaf the 8192 x 8192 matrix read from front is symmetric positive definite. Entry [l, e] names the parent tile joined by tile 8 + e of child l; no row repeats a value. The parent tile q = tile_map[l, e] has (q mod 16 + col_shift[q // 16]) mod 16 equal to (8 + e) mod 16. Among the tiles of one child whose indices are equal mod 8, at most 1 have parent tiles equal mod 16.
All inputs are finite; a program needn't handle non-finite values.
Results may differ from the reference program's by a relative error of at most 0.0001.
Values sent between devices are 32-bit elements; how exact they have to be, the bound alone decides.
No kernel may reach another device: no remote copies, remote signals or barrier semaphores. Data moves between devices by JAX's collectives and lax.ppermute only.
A program may use at most 128 MiB of HBM per device.

```python
import jax
import jax.numpy as jnp
from jax import lax

F = 8192
TILE = 128
PB = 512
PANELS = 2
NPIV = 1024
PRS = 4
PCS = 4
N_LEAF = 2
N_ROW = 8
N_COL = 16


def draw_front(key, part):
    subkeys = jax.random.split(jax.random.fold_in(key, 7), 3)
    factor_width = 4 * PB
    factors = jax.random.normal(subkeys[0], (N_LEAF, F, factor_width), jnp.float32)
    scales = jnp.exp(jax.random.uniform(subkeys[1], (N_LEAF, F), jnp.float32, jnp.log(0.5), jnp.log(2.0)))
    shifts = jnp.exp(jax.random.uniform(subkeys[2], (N_LEAF, F), jnp.float32, jnp.log(0.5), jnp.log(2.0)))
    scaled = factors * (scales / jnp.sqrt(jnp.float32(factor_width)))[:, :, None]
    gram_part = jnp.einsum('lip,ljp->lij', scaled, scaled, precision=lax.Precision.HIGHEST)
    diagonal_ids = jnp.arange(F)
    matrix = gram_part.at[:, diagonal_ids, diagonal_ids].add(shifts)
    return matrix.reshape(N_LEAF, F // (TILE * N_ROW), N_ROW, TILE, F // (TILE * N_COL), N_COL, TILE)


def assembly_maps(key):
    tile_count = F // TILE
    pivot_tiles = NPIV // TILE
    column_slots = tile_count // N_COL
    repeats = (column_slots + N_ROW - 1) // N_ROW
    shift_pool = jnp.arange(repeats * N_ROW, dtype=jnp.int32) % N_ROW
    shuffled = jax.random.permutation(jax.random.fold_in(key, 31), shift_pool)
    col_shift = shuffled[:column_slots].astype(jnp.int32)
    tile_maps = []
    for leaf_index in range(N_LEAF):
        score_key = jax.random.fold_in(key, 41 + leaf_index)
        scores = jax.random.randint(score_key, (N_COL, column_slots), 0, 1 << 20, dtype=jnp.int32) * column_slots + jnp.arange(column_slots, dtype=jnp.int32)[None, :]
        ordering = jnp.argsort(scores, axis=1, stable=True).astype(jnp.int32)
        child_tiles = jnp.arange(pivot_tiles, tile_count, dtype=jnp.int32)
        column_owner = child_tiles % N_COL
        column_slot = child_tiles // N_COL
        parent_slot = ordering[column_owner, column_slot]
        tile_maps.append(N_COL * parent_slot + (column_owner - col_shift[parent_slot]) % N_COL)
    return (jnp.stack(tile_maps).astype(jnp.int32), col_shift)


def draw_tile_map(key, part):
    return assembly_maps(key)[0]


def draw_col_shift(key, part):
    return assembly_maps(key)[1]


def block_levels(key, dims, cuts, low, high):
    def one(axis_at, shards_of):
        heights = jax.random.uniform(jax.random.fold_in(jax.random.fold_in(key, 6), axis_at), (shards_of,), jnp.float32, low / len(cuts), high / len(cuts))
        return jnp.repeat(jnp.exp(heights), dims[axis_at] // shards_of).reshape((-1,) + (1,) * (len(dims) - axis_at - 1))

    level = one(*cuts[0])
    for cut in cuts[1:]:
        level = level * one(*cut)
    return level


def centred(stream_key, shape, deviation, reach, cuts=(), kind=jnp.bfloat16):
    values = deviation * jax.random.normal(stream_key, shape, jnp.float32)
    if cuts:
        values = values * block_levels(stream_key, shape, cuts, -0.22, 0.18)
    return jnp.clip(values, -reach, reach).astype(kind)


def setup_inputs(seed: int = 0) -> dict:
    key_list = jax.random.split(jax.random.key(seed), 5)
    front = draw_front(jax.random.fold_in(key_list[4], 71), 0)
    parent = centred(key_list[1], (PRS, N_LEAF, N_ROW, TILE, PCS, N_COL, TILE), 0.03, 0.2, ((1, 2), (2, 8), (5, 16)), jnp.float32)
    tile_map = draw_tile_map(jax.random.fold_in(key_list[4], 71), 0)
    col_shift = draw_col_shift(jax.random.fold_in(key_list[4], 71), 0)
    return {"front": front, "parent": parent, "tile_map": tile_map, "col_shift": col_shift}


def factor_leaf(matrix):
    for panel_index in range(PANELS):
        panel_start = panel_index * PB
        panel_end = panel_start + PB
        lower_factor = jnp.linalg.cholesky(matrix[panel_start:panel_end, panel_start:panel_end])
        below_panel = lax.linalg.triangular_solve(lower_factor, matrix[panel_end:, panel_start:panel_end], left_side=False, lower=True, transpose_a=True)
        product = jnp.dot(below_panel.astype(jnp.float32), below_panel.T.astype(jnp.float32), precision=lax.Precision.HIGHEST, preferred_element_type=jnp.float32)
        matrix = matrix.at[panel_end:, panel_end:].add(-product)
        matrix = matrix.at[panel_start:panel_end, panel_start:panel_end].set(lower_factor)
        matrix = matrix.at[panel_end:, panel_start:panel_end].set(below_panel)
    row_ids = jnp.arange(F, dtype=jnp.int32)[:, None]
    col_ids = jnp.arange(F, dtype=jnp.int32)[None, :]
    kept_mask = (col_ids < NPIV) & (row_ids >= col_ids) | (col_ids >= NPIV) & (row_ids >= NPIV)
    return jnp.where(kept_mask, matrix, jnp.zeros_like(matrix))

def reference(front, parent, tile_map, col_shift):
    tile_count = F // TILE
    contrib_tiles = tile_count - NPIV // TILE
    full_fronts = front.reshape(N_LEAF, F, F)
    assembled = jnp.zeros((tile_count, TILE, tile_count, TILE), jnp.float32)
    factored_list = []
    for leaf_index in range(N_LEAF):
        factored_leaf = factor_leaf(full_fronts[leaf_index])
        factored_list.append(factored_leaf)
        contribution = factored_leaf[NPIV:, NPIV:].reshape(contrib_tiles, TILE, contrib_tiles, TILE).transpose(0, 2, 1, 3)
        targets = tile_map[leaf_index].astype(jnp.int32)
        assembled = assembled.at[targets[:, None], :, targets[None, :], :].add(contribution)
    factored = jnp.stack(factored_list).reshape(front.shape)
    slot_of_tile = (jnp.arange(tile_count, dtype=jnp.int32) // N_COL).astype(jnp.int32)
    owners = (jnp.arange(tile_count, dtype=jnp.int32) % N_COL).astype(jnp.int32)
    source = (slot_of_tile * N_COL + (owners - col_shift[slot_of_tile]) % N_COL).astype(jnp.int32)
    stored = jnp.take(assembled, source, axis=2)
    new_parent = parent + stored.reshape(parent.shape)
    return (factored, new_parent)
```

```python
import jax
import jax.numpy as jnp
from jax import lax
from jax.sharding import PartitionSpec as P

TILE = 128
PB = 512
PANELS = 2
NPIV = 1024


HIGHEST = lax.Precision.HIGHEST


def spread(value, axis, source):
    kept = jnp.where(lax.axis_index(axis) == source, value, 0).astype(value.dtype)
    return lax.psum(kept, axis)


def update_slots(working, next_rows, column_factor, slot_low, slot_high):
    product = jnp.einsum(
        "atp,bsp->atbs",
        next_rows,
        column_factor,
        precision=HIGHEST,
        preferred_element_type=jnp.float32,
    )
    return working.at[:, :, slot_low:slot_high, :].add(-product)


def per_device(front, parent, tile_map, col_shift):
    leaf_count = lax.axis_size("leaf")
    row_count = lax.axis_size("row")
    col_count = lax.axis_size("col")
    leaf_index = lax.axis_index("leaf")
    row_index = lax.axis_index("row")
    col_index = lax.axis_index("col")
    local_front = front[0, :, 0, :, :, 0, :]
    row_slots = local_front.shape[0]
    col_slots = local_front.shape[2]
    pivot_tiles = NPIV // TILE
    assert pivot_tiles == row_count and pivot_tiles <= col_count
    row_tiles = jnp.arange(row_slots, dtype=jnp.int32) * row_count + row_index
    col_tiles = jnp.arange(col_slots, dtype=jnp.int32) * col_count + col_index

    working = local_front
    top_rows = lax.all_gather(working[0], "row", axis=0, tiled=False)
    column_panel = top_rows.transpose(2, 3, 0, 1).reshape(col_slots, TILE, NPIV)
    first_cols = lax.all_gather(working[:, :, 0, :], "col", axis=0, tiled=False)
    row_panel = first_cols[:pivot_tiles].transpose(1, 2, 0, 3).reshape(row_slots, TILE, NPIV)
    diagonal_block = lax.all_gather(row_panel[0], "row", axis=0, tiled=True)
    lower_factor = jnp.linalg.cholesky(diagonal_block)
    stacked = jnp.concatenate(
        [row_panel[1:].reshape(-1, NPIV), column_panel.reshape(-1, NPIV)], axis=0
    )
    solved = lax.linalg.triangular_solve(
        lower_factor, stacked, left_side=False, lower=True, transpose_a=True
    )
    trailing_rows = (row_slots - 1) * TILE
    row_factor = solved[:trailing_rows].reshape(row_slots - 1, TILE, NPIV)
    column_factor = solved[trailing_rows:].reshape(col_slots, TILE, NPIV)
    column_factor = jnp.where(
        (col_tiles >= pivot_tiles)[:, None, None], column_factor, 0.0
    )
    product = jnp.einsum(
        "atk,bsk->atbs",
        row_factor,
        column_factor,
        precision=HIGHEST,
        preferred_element_type=jnp.float32,
    )
    trailing = working[1:] - product
    own_col = jnp.minimum(col_index, pivot_tiles - 1)
    row_factor_cols = lax.dynamic_slice_in_dim(row_factor, own_col * TILE, TILE, 2)
    is_factor_col = (col_tiles < pivot_tiles)[None, None, :, None]
    trailing = jnp.where(is_factor_col, row_factor_cols[:, :, None, :], trailing)
    diag_rows = lax.dynamic_slice_in_dim(lower_factor, row_index * TILE, TILE, 0)
    diag_tile = lax.dynamic_slice_in_dim(diag_rows, own_col * TILE, TILE, 1)
    local_ids = jnp.arange(TILE, dtype=jnp.int32)
    global_row = row_index * TILE + local_ids[:, None]
    global_col = own_col * TILE + local_ids[None, :]
    diag_tile = jnp.where(global_row >= global_col, diag_tile, 0.0)
    top = jnp.where(is_factor_col[0], diag_tile[:, None, :], 0.0)
    top = jnp.broadcast_to(top, working[0].shape)
    working = jnp.concatenate([top[None], trailing], axis=0)
    factored = working.reshape(front.shape)
    contribution = jnp.where((col_tiles >= pivot_tiles)[None, None, :, None], working, 0.0)
    contrib_count = tile_map.shape[1]
    entry_ids = jnp.arange(contrib_count, dtype=jnp.int32)
    own_map = lax.dynamic_index_in_dim(tile_map, leaf_index, 0, keepdims=False)
    row_match = (row_tiles - pivot_tiles)[:, None] == entry_ids[None, :]
    row_targets = jnp.sum(jnp.where(row_match, own_map[None, :], 0), axis=1)
    row_valid = row_tiles >= pivot_tiles
    owner_count = leaf_count * row_count
    destination = row_targets % owner_count
    parent_row_slot = row_targets // owner_count
    slot_ids = jnp.arange(row_slots, dtype=jnp.int32)
    same_before = (
        (destination[None, :] == destination[:, None])
        & row_valid[None, :]
        & (slot_ids[None, :] < slot_ids[:, None])
    )
    rank_in_dest = jnp.sum(same_before.astype(jnp.int32), axis=1)
    capacity = (col_slots + row_count - 1) // row_count
    owner_ids = jnp.arange(owner_count, dtype=jnp.int32)
    capacity_ids = jnp.arange(capacity, dtype=jnp.int32)
    selection = (
        row_valid[None, None, :]
        & (destination[None, None, :] == owner_ids[:, None, None])
        & (rank_in_dest[None, None, :] == capacity_ids[None, :, None])
    )
    flattened = contribution.reshape(row_slots, -1)
    send_buffer = jnp.einsum(
        "oka,ax->okx",
        selection.astype(jnp.float32),
        flattened,
        precision=HIGHEST,
        preferred_element_type=jnp.float32,
    )
    chosen_slot = jnp.sum(jnp.where(selection, parent_row_slot[None, None, :], 0), axis=2)
    send_slots = jnp.where(jnp.any(selection, axis=2), chosen_slot, -1)
    received, received_slots = (
        lax.all_to_all(send_buffer, ("leaf", "row"), split_axis=0, concat_axis=0, tiled=True),
        lax.all_to_all(send_slots, ("leaf", "row"), split_axis=0, concat_axis=0, tiled=True),
    )
    received = received.reshape(leaf_count, row_count, capacity, -1)
    received_slots = received_slots.reshape(leaf_count, row_count, capacity)
    parent_local = parent[:, 0, 0, :, :, 0, :]
    parent_rows = parent_local.shape[0]
    parent_cols = parent_local.shape[2]
    row_place = (
        received_slots[None] == jnp.arange(parent_rows, dtype=jnp.int32)[:, None, None, None]
    ).astype(jnp.float32)
    by_leaf = jnp.einsum(
        "slrk,lrkx->slx", row_place, received, precision=HIGHEST, preferred_element_type=jnp.float32
    )
    by_leaf = by_leaf.reshape(parent_rows, leaf_count, TILE, col_slots, TILE)
    col_match = (col_tiles - pivot_tiles)[:, None] == entry_ids[None, :]
    col_targets = jnp.sum(jnp.where(col_match[None], tile_map[:, None, :], 0), axis=2)
    col_valid = col_tiles >= pivot_tiles
    parent_slot_ids = jnp.arange(parent_cols, dtype=jnp.int32)
    col_place = (
        col_valid[None, None, :]
        & (col_targets[:, None, :] // col_count == parent_slot_ids[None, :, None])
    ).astype(jnp.float32)
    assembled = jnp.einsum(
        "sltbv,lub->stuv", by_leaf, col_place, precision=HIGHEST, preferred_element_type=jnp.float32
    )
    new_parent = (parent_local + assembled).reshape(parent.shape)
    return (factored, new_parent)


def solution(mesh):
    return jax.shard_map(
        per_device,
        mesh=mesh,
        in_specs=(
            P("leaf", None, "row", None, None, "col", None),
            P(None, "leaf", "row", None, None, "col", None),
            P(),
            P(),
        ),
        out_specs=(
            P("leaf", None, "row", None, None, "col", None),
            P(None, "leaf", "row", None, None, "col", None),
        ),
        check_vma=False,
    )
```

```python
import jax
import jax.numpy as jnp
from jax import lax
from jax.sharding import PartitionSpec as P

TILE = 128
PB = 512
PANELS = 2
NPIV = 1024


HIGHEST = lax.Precision.HIGHEST


def spread(value, axis, source):
    kept = jnp.where(lax.axis_index(axis) == source, value, 0).astype(value.dtype)
    return lax.psum(kept, axis)


def update_slots(working, next_rows, column_factor, slot_low, slot_high):
    product = jnp.einsum(
        "atp,bsp->atbs",
        next_rows,
        column_factor,
        precision=HIGHEST,
        preferred_element_type=jnp.float32,
    )
    return working.at[:, :, slot_low:slot_high, :].add(-product)


def tall_cholesky(diagonal_block, below_rows):
    size = diagonal_block.shape[0]
    remaining = jnp.concatenate([diagonal_block, below_rows], axis=0)
    eye = jnp.eye(TILE, dtype=jnp.float32)
    diag_columns = []
    below_columns = []
    for step in range(size // TILE):
        low = step * TILE
        left = size - low - TILE
        pivot = remaining[:TILE, :TILE]
        pivot_factor = jnp.linalg.cholesky(pivot)
        pivot_inverse = lax.linalg.triangular_solve(
            pivot_factor, eye, left_side=True, lower=True
        )
        under = remaining[TILE:, :TILE]
        solved = jnp.dot(
            under, pivot_inverse.T, precision=HIGHEST, preferred_element_type=jnp.float32
        )
        diag_columns.append(jnp.concatenate([jnp.zeros((low, TILE), jnp.float32), pivot_factor, solved[:left]], axis=0))
        below_columns.append(solved[left:])
        if left:
            update = jnp.dot(
                solved, solved[:left].T, precision=HIGHEST, preferred_element_type=jnp.float32
            )
            remaining = remaining[TILE:, TILE:] - update
    lower_factor = jnp.concatenate(diag_columns, axis=1)
    return lower_factor, jnp.concatenate(below_columns, axis=1)


def per_device(front, parent, tile_map, col_shift):
    leaf_count = lax.axis_size("leaf")
    row_count = lax.axis_size("row")
    col_count = lax.axis_size("col")
    leaf_index = lax.axis_index("leaf")
    row_index = lax.axis_index("row")
    col_index = lax.axis_index("col")
    local_front = front[0, :, 0, :, :, 0, :]
    row_slots = local_front.shape[0]
    col_slots = local_front.shape[2]
    pivot_tiles = NPIV // TILE
    assert pivot_tiles == row_count and pivot_tiles <= col_count
    row_tiles = jnp.arange(row_slots, dtype=jnp.int32) * row_count + row_index
    col_tiles = jnp.arange(col_slots, dtype=jnp.int32) * col_count + col_index

    working = local_front
    first_tiles = lax.all_gather(working[0, :, 0, :], "col", axis=0, tiled=False)
    diag_row = first_tiles[:pivot_tiles].transpose(1, 0, 2).reshape(TILE, NPIV)
    diagonal_block = lax.all_gather(diag_row, "row", axis=0, tiled=True)
    rest_cols, top_input, diagonal_block = lax.optimization_barrier(
        (working[1:, :, 0, :], working[0], diagonal_block)
    )
    first_cols = lax.all_gather(rest_cols, "col", axis=0, tiled=False)
    row_panel = first_cols[:pivot_tiles].transpose(1, 2, 0, 3).reshape(row_slots - 1, TILE, NPIV)
    top_rows = lax.all_gather(top_input, "row", axis=0, tiled=False)
    column_panel = top_rows.transpose(2, 3, 0, 1).reshape(col_slots, TILE, NPIV)
    stacked = jnp.concatenate(
        [row_panel.reshape(-1, NPIV), column_panel.reshape(-1, NPIV)], axis=0
    )
    lower_factor, solved = tall_cholesky(diagonal_block, stacked)
    trailing_rows = (row_slots - 1) * TILE
    row_factor = solved[:trailing_rows].reshape(row_slots - 1, TILE, NPIV)
    column_factor = solved[trailing_rows:].reshape(col_slots, TILE, NPIV)
    column_factor = jnp.where(
        (col_tiles >= pivot_tiles)[:, None, None], column_factor, 0.0
    )
    product = jnp.einsum(
        "atk,bsk->atbs",
        row_factor,
        column_factor,
        precision=HIGHEST,
        preferred_element_type=jnp.float32,
    )
    trailing = working[1:] - product
    own_col = jnp.minimum(col_index, pivot_tiles - 1)
    row_factor_cols = lax.dynamic_slice_in_dim(row_factor, own_col * TILE, TILE, 2)
    is_factor_col = (col_tiles < pivot_tiles)[None, None, :, None]
    trailing = jnp.where(is_factor_col, row_factor_cols[:, :, None, :], trailing)
    diag_rows = lax.dynamic_slice_in_dim(lower_factor, row_index * TILE, TILE, 0)
    diag_tile = lax.dynamic_slice_in_dim(diag_rows, own_col * TILE, TILE, 1)
    local_ids = jnp.arange(TILE, dtype=jnp.int32)
    global_row = row_index * TILE + local_ids[:, None]
    global_col = own_col * TILE + local_ids[None, :]
    diag_tile = jnp.where(global_row >= global_col, diag_tile, 0.0)
    top = jnp.where(is_factor_col[0], diag_tile[:, None, :], 0.0)
    top = jnp.broadcast_to(top, working[0].shape)
    working = jnp.concatenate([top[None], trailing], axis=0)
    factored = working.reshape(front.shape)
    contribution = jnp.where((col_tiles >= pivot_tiles)[None, None, :, None], working, 0.0)
    contrib_count = tile_map.shape[1]
    entry_ids = jnp.arange(contrib_count, dtype=jnp.int32)
    own_map = lax.dynamic_index_in_dim(tile_map, leaf_index, 0, keepdims=False)
    row_match = (row_tiles - pivot_tiles)[:, None] == entry_ids[None, :]
    row_targets = jnp.sum(jnp.where(row_match, own_map[None, :], 0), axis=1)
    row_valid = row_tiles >= pivot_tiles
    owner_count = leaf_count * row_count
    destination = row_targets % owner_count
    parent_row_slot = row_targets // owner_count
    slot_ids = jnp.arange(row_slots, dtype=jnp.int32)
    same_before = (
        (destination[None, :] == destination[:, None])
        & row_valid[None, :]
        & (slot_ids[None, :] < slot_ids[:, None])
    )
    rank_in_dest = jnp.sum(same_before.astype(jnp.int32), axis=1)
    capacity = (col_slots + row_count - 1) // row_count
    owner_ids = jnp.arange(owner_count, dtype=jnp.int32)
    capacity_ids = jnp.arange(capacity, dtype=jnp.int32)
    selection = (
        row_valid[None, None, :]
        & (destination[None, None, :] == owner_ids[:, None, None])
        & (rank_in_dest[None, None, :] == capacity_ids[None, :, None])
    )
    flattened = contribution.reshape(row_slots, -1)
    send_buffer = jnp.einsum(
        "oka,ax->okx",
        selection.astype(jnp.float32),
        flattened,
        precision=HIGHEST,
        preferred_element_type=jnp.float32,
    )
    chosen_slot = jnp.sum(jnp.where(selection, parent_row_slot[None, None, :], 0), axis=2)
    send_slots = jnp.where(jnp.any(selection, axis=2), chosen_slot, -1)
    received, received_slots = (
        lax.all_to_all(send_buffer, ("leaf", "row"), split_axis=0, concat_axis=0, tiled=True),
        lax.all_to_all(send_slots, ("leaf", "row"), split_axis=0, concat_axis=0, tiled=True),
    )
    received = received.reshape(leaf_count, row_count, capacity, -1)
    received_slots = received_slots.reshape(leaf_count, row_count, capacity)
    parent_local = parent[:, 0, 0, :, :, 0, :]
    parent_rows = parent_local.shape[0]
    parent_cols = parent_local.shape[2]
    row_place = (
        received_slots[None] == jnp.arange(parent_rows, dtype=jnp.int32)[:, None, None, None]
    ).astype(jnp.float32)
    by_leaf = jnp.einsum(
        "slrk,lrkx->slx", row_place, received, precision=HIGHEST, preferred_element_type=jnp.float32
    )
    by_leaf = by_leaf.reshape(parent_rows, leaf_count, TILE, col_slots, TILE)
    col_match = (col_tiles - pivot_tiles)[:, None] == entry_ids[None, :]
    col_targets = jnp.sum(jnp.where(col_match[None], tile_map[:, None, :], 0), axis=2)
    col_valid = col_tiles >= pivot_tiles
    parent_slot_ids = jnp.arange(parent_cols, dtype=jnp.int32)
    col_place = (
        col_valid[None, None, :]
        & (col_targets[:, None, :] // col_count == parent_slot_ids[None, :, None])
    ).astype(jnp.float32)
    assembled = jnp.einsum(
        "sltbv,lub->stuv", by_leaf, col_place, precision=HIGHEST, preferred_element_type=jnp.float32
    )
    new_parent = (parent_local + assembled).reshape(parent.shape)
    return (factored, new_parent)


def solution(mesh):
    return jax.shard_map(
        per_device,
        mesh=mesh,
        in_specs=(
            P("leaf", None, "row", None, None, "col", None),
            P(None, "leaf", "row", None, None, "col", None),
            P(),
            P(),
        ),
        out_specs=(
            P("leaf", None, "row", None, None, "col", None),
            P(None, "leaf", "row", None, None, "col", None),
        ),
        check_vma=False,
    )
```

```python
import jax
import jax.numpy as jnp
from jax import lax
from jax.sharding import PartitionSpec as P

TILE = 128
PB = 512
PANELS = 2
NPIV = 1024


HIGHEST = lax.Precision.HIGHEST


def spread(value, axis, source):
    kept = jnp.where(lax.axis_index(axis) == source, value, 0).astype(value.dtype)
    return lax.psum(kept, axis)


def update_slots(working, next_rows, column_factor, slot_low, slot_high):
    product = jnp.einsum(
        "atp,bsp->atbs",
        next_rows,
        column_factor,
        precision=HIGHEST,
        preferred_element_type=jnp.float32,
    )
    return working.at[:, :, slot_low:slot_high, :].add(-product)


def tall_cholesky(diagonal_block, below_rows):
    size = diagonal_block.shape[0]
    remaining = diagonal_block
    eye = jnp.eye(TILE, dtype=jnp.float32)
    diag_columns = []
    inverses = []
    for step in range(size // TILE):
        low = step * TILE
        left = size - low - TILE
        pivot = remaining[:TILE, :TILE]
        pivot_factor = jnp.linalg.cholesky(pivot)
        pivot_inverse = lax.linalg.triangular_solve(
            pivot_factor, eye, left_side=True, lower=True
        )
        inverses.append(pivot_inverse)
        parts = [jnp.zeros((low, TILE), jnp.float32), pivot_factor]
        if left:
            solved = jnp.dot(
                remaining[TILE:, :TILE],
                pivot_inverse.T,
                precision=HIGHEST,
                preferred_element_type=jnp.float32,
            )
            parts.append(solved)
            update = jnp.dot(
                solved, solved.T, precision=HIGHEST, preferred_element_type=jnp.float32
            )
            remaining = remaining[TILE:, TILE:] - update
        diag_columns.append(jnp.concatenate(parts, axis=0))
    lower_factor = jnp.concatenate(diag_columns, axis=1)
    rest = below_rows
    below_columns = []
    for step in range(size // TILE):
        low = step * TILE
        solved = jnp.dot(
            rest[:, :TILE], inverses[step].T, precision=HIGHEST, preferred_element_type=jnp.float32
        )
        below_columns.append(solved)
        if low + TILE < size:
            update = jnp.dot(
                solved,
                lower_factor[low + TILE :, low : low + TILE].T,
                precision=HIGHEST,
                preferred_element_type=jnp.float32,
            )
            rest = rest[:, TILE:] - update
    return lower_factor, jnp.concatenate(below_columns, axis=1)

def per_device(front, parent, tile_map, col_shift):
    leaf_count = lax.axis_size("leaf")
    row_count = lax.axis_size("row")
    col_count = lax.axis_size("col")
    leaf_index = lax.axis_index("leaf")
    row_index = lax.axis_index("row")
    col_index = lax.axis_index("col")
    local_front = front[0, :, 0, :, :, 0, :]
    row_slots = local_front.shape[0]
    col_slots = local_front.shape[2]
    pivot_tiles = NPIV // TILE
    assert pivot_tiles == row_count and pivot_tiles <= col_count
    row_tiles = jnp.arange(row_slots, dtype=jnp.int32) * row_count + row_index
    col_tiles = jnp.arange(col_slots, dtype=jnp.int32) * col_count + col_index

    working = local_front
    first_tiles = lax.all_gather(working[0, :, 0, :], "col", axis=0, tiled=False)
    diag_row = first_tiles[:pivot_tiles].transpose(1, 0, 2).reshape(TILE, NPIV)
    diagonal_block = lax.all_gather(diag_row, "row", axis=0, tiled=True)
    rest_cols, top_input, diagonal_block = lax.optimization_barrier(
        (working[1:, :, 0, :], working[0], diagonal_block)
    )
    first_cols = lax.all_gather(rest_cols, "col", axis=0, tiled=False)
    row_panel = first_cols[:pivot_tiles].transpose(1, 2, 0, 3).reshape(row_slots - 1, TILE, NPIV)
    top_rows = lax.all_gather(top_input, "row", axis=0, tiled=False)
    column_panel = top_rows.transpose(2, 3, 0, 1).reshape(col_slots, TILE, NPIV)
    stacked = jnp.concatenate(
        [row_panel.reshape(-1, NPIV), column_panel.reshape(-1, NPIV)], axis=0
    )
    lower_factor, solved = tall_cholesky(diagonal_block, stacked)
    trailing_rows = (row_slots - 1) * TILE
    row_factor = solved[:trailing_rows].reshape(row_slots - 1, TILE, NPIV)
    column_factor = solved[trailing_rows:].reshape(col_slots, TILE, NPIV)
    column_factor = jnp.where(
        (col_tiles >= pivot_tiles)[:, None, None], column_factor, 0.0
    )
    product = jnp.einsum(
        "atk,bsk->atbs",
        row_factor,
        column_factor,
        precision=HIGHEST,
        preferred_element_type=jnp.float32,
    )
    trailing = working[1:] - product
    own_col = jnp.minimum(col_index, pivot_tiles - 1)
    row_factor_cols = lax.dynamic_slice_in_dim(row_factor, own_col * TILE, TILE, 2)
    is_factor_col = (col_tiles < pivot_tiles)[None, None, :, None]
    trailing = jnp.where(is_factor_col, row_factor_cols[:, :, None, :], trailing)
    diag_rows = lax.dynamic_slice_in_dim(lower_factor, row_index * TILE, TILE, 0)
    diag_tile = lax.dynamic_slice_in_dim(diag_rows, own_col * TILE, TILE, 1)
    local_ids = jnp.arange(TILE, dtype=jnp.int32)
    global_row = row_index * TILE + local_ids[:, None]
    global_col = own_col * TILE + local_ids[None, :]
    diag_tile = jnp.where(global_row >= global_col, diag_tile, 0.0)
    top = jnp.where(is_factor_col[0], diag_tile[:, None, :], 0.0)
    top = jnp.broadcast_to(top, working[0].shape)
    working = jnp.concatenate([top[None], trailing], axis=0)
    factored = working.reshape(front.shape)
    contribution = jnp.where((col_tiles >= pivot_tiles)[None, None, :, None], working, 0.0)
    contrib_count = tile_map.shape[1]
    entry_ids = jnp.arange(contrib_count, dtype=jnp.int32)
    own_map = lax.dynamic_index_in_dim(tile_map, leaf_index, 0, keepdims=False)
    row_match = (row_tiles - pivot_tiles)[:, None] == entry_ids[None, :]
    row_targets = jnp.sum(jnp.where(row_match, own_map[None, :], 0), axis=1)
    row_valid = row_tiles >= pivot_tiles
    owner_count = leaf_count * row_count
    destination = row_targets % owner_count
    parent_row_slot = row_targets // owner_count
    slot_ids = jnp.arange(row_slots, dtype=jnp.int32)
    same_before = (
        (destination[None, :] == destination[:, None])
        & row_valid[None, :]
        & (slot_ids[None, :] < slot_ids[:, None])
    )
    rank_in_dest = jnp.sum(same_before.astype(jnp.int32), axis=1)
    capacity = (col_slots + row_count - 1) // row_count
    owner_ids = jnp.arange(owner_count, dtype=jnp.int32)
    capacity_ids = jnp.arange(capacity, dtype=jnp.int32)
    selection = (
        row_valid[None, None, :]
        & (destination[None, None, :] == owner_ids[:, None, None])
        & (rank_in_dest[None, None, :] == capacity_ids[None, :, None])
    )
    flattened = contribution.reshape(row_slots, -1)
    send_buffer = jnp.einsum(
        "oka,ax->okx",
        selection.astype(jnp.float32),
        flattened,
        precision=HIGHEST,
        preferred_element_type=jnp.float32,
    )
    chosen_slot = jnp.sum(jnp.where(selection, parent_row_slot[None, None, :], 0), axis=2)
    send_slots = jnp.where(jnp.any(selection, axis=2), chosen_slot, -1)
    received, received_slots = (
        lax.all_to_all(send_buffer, ("leaf", "row"), split_axis=0, concat_axis=0, tiled=True),
        lax.all_to_all(send_slots, ("leaf", "row"), split_axis=0, concat_axis=0, tiled=True),
    )
    received = received.reshape(leaf_count, row_count, capacity, -1)
    received_slots = received_slots.reshape(leaf_count, row_count, capacity)
    parent_local = parent[:, 0, 0, :, :, 0, :]
    parent_rows = parent_local.shape[0]
    parent_cols = parent_local.shape[2]
    row_place = (
        received_slots[None] == jnp.arange(parent_rows, dtype=jnp.int32)[:, None, None, None]
    ).astype(jnp.float32)
    by_leaf = jnp.einsum(
        "slrk,lrkx->slx", row_place, received, precision=HIGHEST, preferred_element_type=jnp.float32
    )
    by_leaf = by_leaf.reshape(parent_rows, leaf_count, TILE, col_slots, TILE)
    col_match = (col_tiles - pivot_tiles)[:, None] == entry_ids[None, :]
    col_targets = jnp.sum(jnp.where(col_match[None], tile_map[:, None, :], 0), axis=2)
    col_valid = col_tiles >= pivot_tiles
    parent_slot_ids = jnp.arange(parent_cols, dtype=jnp.int32)
    col_place = (
        col_valid[None, None, :]
        & (col_targets[:, None, :] // col_count == parent_slot_ids[None, :, None])
    ).astype(jnp.float32)
    assembled = jnp.einsum(
        "sltbv,lub->stuv", by_leaf, col_place, precision=HIGHEST, preferred_element_type=jnp.float32
    )
    new_parent = (parent_local + assembled).reshape(parent.shape)
    return (factored, new_parent)


def solution(mesh):
    return jax.shard_map(
        per_device,
        mesh=mesh,
        in_specs=(
            P("leaf", None, "row", None, None, "col", None),
            P(None, "leaf", "row", None, None, "col", None),
            P(),
            P(),
        ),
        out_specs=(
            P("leaf", None, "row", None, None, "col", None),
            P(None, "leaf", "row", None, None, "col", None),
        ),
        check_vma=False,
    )
```

```python
import jax
import jax.numpy as jnp
from jax import lax
from jax.sharding import PartitionSpec as P
from jax.experimental import pallas as pl
from jax.experimental.pallas import tpu as pltpu

TILE = 128
PB = 512
PANELS = 2
NPIV = 1024


HIGHEST = lax.Precision.HIGHEST


def spread(value, axis, source):
    kept = jnp.where(lax.axis_index(axis) == source, value, 0).astype(value.dtype)
    return lax.psum(kept, axis)


def update_slots(working, next_rows, column_factor, slot_low, slot_high):
    product = jnp.einsum(
        "atp,bsp->atbs",
        next_rows,
        column_factor,
        precision=HIGHEST,
        preferred_element_type=jnp.float32,
    )
    return working.at[:, :, slot_low:slot_high, :].add(-product)


def _chol_inverse_kernel(a_ref, l_ref, x_ref, a_scr, x_scr, lt_scr):
    size = a_ref.shape[0]
    block = a_ref[...]
    a_scr[...] = 0.5 * (block + block.T)
    lanes = lax.broadcasted_iota(jnp.int32, (size, size), 1)
    subs = lax.broadcasted_iota(jnp.int32, (size, size), 0)
    x_scr[...] = jnp.where(lanes == subs, 1.0, 0.0).astype(jnp.float32)
    lt_scr[...] = jnp.zeros((size, size), jnp.float32)
    col_ids = lax.broadcasted_iota(jnp.int32, (size, 1), 0)
    row_ids = lax.broadcasted_iota(jnp.int32, (1, size), 1)

    def body(j, carry):
        current = a_scr[...]
        row = a_scr[pl.ds(j, 1), :]
        pivot = jnp.sum(jnp.where(row_ids == j, row, 0.0), axis=1, keepdims=True)
        root = jnp.sqrt(pivot)
        l_row = jnp.where(row_ids > j, row / root, 0.0)
        l_row = jnp.where(row_ids == j, root, l_row)
        column = jnp.sum(jnp.where(lanes == j, current, 0.0), axis=1, keepdims=True)
        l_col = jnp.where(col_ids > j, column / root, 0.0)
        l_col = jnp.where(col_ids == j, root, l_col)
        a_scr[...] = current - l_col * l_row
        lt_scr[pl.ds(j, 1), :] = l_row
        x_row = x_scr[pl.ds(j, 1), :] / root
        strict = jnp.where(col_ids > j, l_col, 0.0)
        x_scr[...] = x_scr[...] - strict * x_row
        x_scr[pl.ds(j, 1), :] = x_row
        return carry

    lax.fori_loop(0, size, body, 0)
    l_ref[...] = lt_scr[...].T
    x_ref[...] = x_scr[...]


def chol_inverse(block):
    size = block.shape[0]
    shape = jax.ShapeDtypeStruct((size, size), jnp.float32)
    return pl.pallas_call(
        _chol_inverse_kernel,
        out_shape=(shape, shape),
        scratch_shapes=[pltpu.VMEM((size, size), jnp.float32)] * 3,
    )(block)


def tall_cholesky(diagonal_block, below_rows):
    size = diagonal_block.shape[0]
    remaining = diagonal_block
    diag_columns = []
    inverses = []
    for step in range(size // TILE):
        low = step * TILE
        left = size - low - TILE
        pivot = remaining[:TILE, :TILE]
        pivot_factor, pivot_inverse = chol_inverse(pivot)
        inverses.append(pivot_inverse)
        parts = [jnp.zeros((low, TILE), jnp.float32), pivot_factor]
        if left:
            solved = jnp.dot(
                remaining[TILE:, :TILE],
                pivot_inverse.T,
                precision=HIGHEST,
                preferred_element_type=jnp.float32,
            )
            parts.append(solved)
            update = jnp.dot(
                solved, solved.T, precision=HIGHEST, preferred_element_type=jnp.float32
            )
            remaining = remaining[TILE:, TILE:] - update
        diag_columns.append(jnp.concatenate(parts, axis=0))
    lower_factor = jnp.concatenate(diag_columns, axis=1)
    rest = below_rows
    below_columns = []
    for step in range(size // TILE):
        low = step * TILE
        solved = jnp.dot(
            rest[:, :TILE], inverses[step].T, precision=HIGHEST, preferred_element_type=jnp.float32
        )
        below_columns.append(solved)
        if low + TILE < size:
            update = jnp.dot(
                solved,
                lower_factor[low + TILE :, low : low + TILE].T,
                precision=HIGHEST,
                preferred_element_type=jnp.float32,
            )
            rest = rest[:, TILE:] - update
    return lower_factor, jnp.concatenate(below_columns, axis=1)

def per_device(front, parent, tile_map, col_shift):
    leaf_count = lax.axis_size("leaf")
    row_count = lax.axis_size("row")
    col_count = lax.axis_size("col")
    leaf_index = lax.axis_index("leaf")
    row_index = lax.axis_index("row")
    col_index = lax.axis_index("col")
    local_front = front[0, :, 0, :, :, 0, :]
    row_slots = local_front.shape[0]
    col_slots = local_front.shape[2]
    pivot_tiles = NPIV // TILE
    assert pivot_tiles == row_count and pivot_tiles <= col_count
    row_tiles = jnp.arange(row_slots, dtype=jnp.int32) * row_count + row_index
    col_tiles = jnp.arange(col_slots, dtype=jnp.int32) * col_count + col_index

    working = local_front
    first_tiles = lax.all_gather(working[0, :, 0, :], "col", axis=0, tiled=False)
    diag_row = first_tiles[:pivot_tiles].transpose(1, 0, 2).reshape(TILE, NPIV)
    diagonal_block = lax.all_gather(diag_row, "row", axis=0, tiled=True)
    rest_cols, top_input, diagonal_block = lax.optimization_barrier(
        (working[1:, :, 0, :], working[0], diagonal_block)
    )
    first_cols = lax.all_gather(rest_cols, "col", axis=0, tiled=False)
    row_panel = first_cols[:pivot_tiles].transpose(1, 2, 0, 3).reshape(row_slots - 1, TILE, NPIV)
    top_rows = lax.all_gather(top_input, "row", axis=0, tiled=False)
    column_panel = top_rows.transpose(2, 3, 0, 1).reshape(col_slots, TILE, NPIV)
    stacked = jnp.concatenate(
        [row_panel.reshape(-1, NPIV), column_panel.reshape(-1, NPIV)], axis=0
    )
    lower_factor, solved = tall_cholesky(diagonal_block, stacked)
    trailing_rows = (row_slots - 1) * TILE
    row_factor = solved[:trailing_rows].reshape(row_slots - 1, TILE, NPIV)
    column_factor = solved[trailing_rows:].reshape(col_slots, TILE, NPIV)
    column_factor = jnp.where(
        (col_tiles >= pivot_tiles)[:, None, None], column_factor, 0.0
    )
    product = jnp.einsum(
        "atk,bsk->atbs",
        row_factor,
        column_factor,
        precision=HIGHEST,
        preferred_element_type=jnp.float32,
    )
    trailing = working[1:] - product
    own_col = jnp.minimum(col_index, pivot_tiles - 1)
    row_factor_cols = lax.dynamic_slice_in_dim(row_factor, own_col * TILE, TILE, 2)
    is_factor_col = (col_tiles < pivot_tiles)[None, None, :, None]
    trailing = jnp.where(is_factor_col, row_factor_cols[:, :, None, :], trailing)
    diag_rows = lax.dynamic_slice_in_dim(lower_factor, row_index * TILE, TILE, 0)
    diag_tile = lax.dynamic_slice_in_dim(diag_rows, own_col * TILE, TILE, 1)
    local_ids = jnp.arange(TILE, dtype=jnp.int32)
    global_row = row_index * TILE + local_ids[:, None]
    global_col = own_col * TILE + local_ids[None, :]
    diag_tile = jnp.where(global_row >= global_col, diag_tile, 0.0)
    top = jnp.where(is_factor_col[0], diag_tile[:, None, :], 0.0)
    top = jnp.broadcast_to(top, working[0].shape)
    working = jnp.concatenate([top[None], trailing], axis=0)
    factored = working.reshape(front.shape)
    contribution = jnp.where((col_tiles >= pivot_tiles)[None, None, :, None], working, 0.0)
    contrib_count = tile_map.shape[1]
    entry_ids = jnp.arange(contrib_count, dtype=jnp.int32)
    own_map = lax.dynamic_index_in_dim(tile_map, leaf_index, 0, keepdims=False)
    row_match = (row_tiles - pivot_tiles)[:, None] == entry_ids[None, :]
    row_targets = jnp.sum(jnp.where(row_match, own_map[None, :], 0), axis=1)
    row_valid = row_tiles >= pivot_tiles
    owner_count = leaf_count * row_count
    destination = row_targets % owner_count
    parent_row_slot = row_targets // owner_count
    slot_ids = jnp.arange(row_slots, dtype=jnp.int32)
    same_before = (
        (destination[None, :] == destination[:, None])
        & row_valid[None, :]
        & (slot_ids[None, :] < slot_ids[:, None])
    )
    rank_in_dest = jnp.sum(same_before.astype(jnp.int32), axis=1)
    capacity = (col_slots + row_count - 1) // row_count
    owner_ids = jnp.arange(owner_count, dtype=jnp.int32)
    capacity_ids = jnp.arange(capacity, dtype=jnp.int32)
    selection = (
        row_valid[None, None, :]
        & (destination[None, None, :] == owner_ids[:, None, None])
        & (rank_in_dest[None, None, :] == capacity_ids[None, :, None])
    )
    flattened = contribution.reshape(row_slots, -1)
    send_buffer = jnp.einsum(
        "oka,ax->okx",
        selection.astype(jnp.float32),
        flattened,
        precision=HIGHEST,
        preferred_element_type=jnp.float32,
    )
    chosen_slot = jnp.sum(jnp.where(selection, parent_row_slot[None, None, :], 0), axis=2)
    send_slots = jnp.where(jnp.any(selection, axis=2), chosen_slot, -1)
    received, received_slots = (
        lax.all_to_all(send_buffer, ("leaf", "row"), split_axis=0, concat_axis=0, tiled=True),
        lax.all_to_all(send_slots, ("leaf", "row"), split_axis=0, concat_axis=0, tiled=True),
    )
    received = received.reshape(leaf_count, row_count, capacity, -1)
    received_slots = received_slots.reshape(leaf_count, row_count, capacity)
    parent_local = parent[:, 0, 0, :, :, 0, :]
    parent_rows = parent_local.shape[0]
    parent_cols = parent_local.shape[2]
    row_place = (
        received_slots[None] == jnp.arange(parent_rows, dtype=jnp.int32)[:, None, None, None]
    ).astype(jnp.float32)
    by_leaf = jnp.einsum(
        "slrk,lrkx->slx", row_place, received, precision=HIGHEST, preferred_element_type=jnp.float32
    )
    by_leaf = by_leaf.reshape(parent_rows, leaf_count, TILE, col_slots, TILE)
    col_match = (col_tiles - pivot_tiles)[:, None] == entry_ids[None, :]
    col_targets = jnp.sum(jnp.where(col_match[None], tile_map[:, None, :], 0), axis=2)
    col_valid = col_tiles >= pivot_tiles
    parent_slot_ids = jnp.arange(parent_cols, dtype=jnp.int32)
    col_place = (
        col_valid[None, None, :]
        & (col_targets[:, None, :] // col_count == parent_slot_ids[None, :, None])
    ).astype(jnp.float32)
    assembled = jnp.einsum(
        "sltbv,lub->stuv", by_leaf, col_place, precision=HIGHEST, preferred_element_type=jnp.float32
    )
    new_parent = (parent_local + assembled).reshape(parent.shape)
    return (factored, new_parent)


def solution(mesh):
    return jax.shard_map(
        per_device,
        mesh=mesh,
        in_specs=(
            P("leaf", None, "row", None, None, "col", None),
            P(None, "leaf", "row", None, None, "col", None),
            P(),
            P(),
        ),
        out_specs=(
            P("leaf", None, "row", None, None, "col", None),
            P(None, "leaf", "row", None, None, "col", None),
        ),
        check_vma=False,
    )
```

```python
import jax
import jax.numpy as jnp
from jax import lax
from jax.sharding import PartitionSpec as P
from jax.experimental import pallas as pl
from jax.experimental.pallas import tpu as pltpu

TILE = 128
PB = 512
PANELS = 2
NPIV = 1024


HIGHEST = lax.Precision.HIGHEST


def spread(value, axis, source):
    kept = jnp.where(lax.axis_index(axis) == source, value, 0).astype(value.dtype)
    return lax.psum(kept, axis)


def update_slots(working, next_rows, column_factor, slot_low, slot_high):
    product = jnp.einsum(
        "atp,bsp->atbs",
        next_rows,
        column_factor,
        precision=HIGHEST,
        preferred_element_type=jnp.float32,
    )
    return working.at[:, :, slot_low:slot_high, :].add(-product)


def _chol_inverse_kernel(a_ref, l_ref, x_ref, a_scr, x_scr, lt_scr):
    size = a_ref.shape[0]
    block = a_ref[...]
    a_scr[...] = 0.5 * (block + block.T)
    lanes = lax.broadcasted_iota(jnp.int32, (size, size), 1)
    subs = lax.broadcasted_iota(jnp.int32, (size, size), 0)
    x_scr[...] = jnp.where(lanes == subs, 1.0, 0.0).astype(jnp.float32)
    lt_scr[...] = jnp.zeros((size, size), jnp.float32)
    row_ids = lax.broadcasted_iota(jnp.int32, (1, size), 1)
    group = 8
    for phase in range(size // group):
        top = phase * group
        active = size - top
        col_ids = lax.broadcasted_iota(jnp.int32, (active, 1), 0) + top
        active_lanes = lax.broadcasted_iota(jnp.int32, (active, size), 1)

        def body(t, carry, top=top, col_ids=col_ids, active_lanes=active_lanes):
            j = top + t
            current = a_scr[top:, :]
            row = a_scr[pl.ds(j, 1), :]
            pivot = jnp.sum(jnp.where(row_ids == j, row, 0.0), axis=1, keepdims=True)
            root = jnp.sqrt(pivot)
            l_row = jnp.where(row_ids > j, row / root, 0.0)
            l_row = jnp.where(row_ids == j, root, l_row)
            column = jnp.sum(
                jnp.where(active_lanes == j, current, 0.0), axis=1, keepdims=True
            )
            l_col = jnp.where(col_ids > j, column / root, 0.0)
            l_col = jnp.where(col_ids == j, root, l_col)
            a_scr[top:, :] = current - l_col * l_row
            lt_scr[pl.ds(j, 1), :] = l_row
            x_row = x_scr[pl.ds(j, 1), :] / root
            strict = jnp.where(col_ids > j, l_col, 0.0)
            x_scr[top:, :] = x_scr[top:, :] - strict * x_row
            x_scr[pl.ds(j, 1), :] = x_row
            return carry

        lax.fori_loop(0, group, body, 0)
    l_ref[...] = lt_scr[...].T
    x_ref[...] = x_scr[...]


def chol_inverse(block):
    size = block.shape[0]
    shape = jax.ShapeDtypeStruct((size, size), jnp.float32)
    return pl.pallas_call(
        _chol_inverse_kernel,
        out_shape=(shape, shape),
        scratch_shapes=[pltpu.VMEM((size, size), jnp.float32)] * 3,
    )(block)


def tall_cholesky(diagonal_block, below_rows):
    size = diagonal_block.shape[0]
    remaining = diagonal_block
    diag_columns = []
    inverses = []
    for step in range(size // TILE):
        low = step * TILE
        left = size - low - TILE
        pivot = remaining[:TILE, :TILE]
        pivot_factor, pivot_inverse = chol_inverse(pivot)
        inverses.append(pivot_inverse)
        parts = [jnp.zeros((low, TILE), jnp.float32), pivot_factor]
        if left:
            solved = jnp.dot(
                remaining[TILE:, :TILE],
                pivot_inverse.T,
                precision=HIGHEST,
                preferred_element_type=jnp.float32,
            )
            parts.append(solved)
            update = jnp.dot(
                solved, solved.T, precision=HIGHEST, preferred_element_type=jnp.float32
            )
            remaining = remaining[TILE:, TILE:] - update
        diag_columns.append(jnp.concatenate(parts, axis=0))
    lower_factor = jnp.concatenate(diag_columns, axis=1)
    rest = below_rows
    below_columns = []
    for step in range(size // TILE):
        low = step * TILE
        solved = jnp.dot(
            rest[:, :TILE], inverses[step].T, precision=HIGHEST, preferred_element_type=jnp.float32
        )
        below_columns.append(solved)
        if low + TILE < size:
            update = jnp.dot(
                solved,
                lower_factor[low + TILE :, low : low + TILE].T,
                precision=HIGHEST,
                preferred_element_type=jnp.float32,
            )
            rest = rest[:, TILE:] - update
    return lower_factor, jnp.concatenate(below_columns, axis=1)

def per_device(front, parent, tile_map, col_shift):
    leaf_count = lax.axis_size("leaf")
    row_count = lax.axis_size("row")
    col_count = lax.axis_size("col")
    leaf_index = lax.axis_index("leaf")
    row_index = lax.axis_index("row")
    col_index = lax.axis_index("col")
    local_front = front[0, :, 0, :, :, 0, :]
    row_slots = local_front.shape[0]
    col_slots = local_front.shape[2]
    pivot_tiles = NPIV // TILE
    assert pivot_tiles == row_count and pivot_tiles <= col_count
    row_tiles = jnp.arange(row_slots, dtype=jnp.int32) * row_count + row_index
    col_tiles = jnp.arange(col_slots, dtype=jnp.int32) * col_count + col_index

    working = local_front
    first_tiles = lax.all_gather(working[0, :, 0, :], "col", axis=0, tiled=False)
    diag_row = first_tiles[:pivot_tiles].transpose(1, 0, 2).reshape(TILE, NPIV)
    diagonal_block = lax.all_gather(diag_row, "row", axis=0, tiled=True)
    rest_cols, top_input, diagonal_block = lax.optimization_barrier(
        (working[1:, :, 0, :], working[0], diagonal_block)
    )
    first_cols = lax.all_gather(rest_cols, "col", axis=0, tiled=False)
    row_panel = first_cols[:pivot_tiles].transpose(1, 2, 0, 3).reshape(row_slots - 1, TILE, NPIV)
    top_rows = lax.all_gather(top_input, "row", axis=0, tiled=False)
    column_panel = top_rows.transpose(2, 3, 0, 1).reshape(col_slots, TILE, NPIV)
    stacked = jnp.concatenate(
        [row_panel.reshape(-1, NPIV), column_panel.reshape(-1, NPIV)], axis=0
    )
    lower_factor, solved = tall_cholesky(diagonal_block, stacked)
    trailing_rows = (row_slots - 1) * TILE
    row_factor = solved[:trailing_rows].reshape(row_slots - 1, TILE, NPIV)
    column_factor = solved[trailing_rows:].reshape(col_slots, TILE, NPIV)
    column_factor = jnp.where(
        (col_tiles >= pivot_tiles)[:, None, None], column_factor, 0.0
    )
    product = jnp.einsum(
        "atk,bsk->atbs",
        row_factor,
        column_factor,
        precision=HIGHEST,
        preferred_element_type=jnp.float32,
    )
    trailing = working[1:] - product
    own_col = jnp.minimum(col_index, pivot_tiles - 1)
    row_factor_cols = lax.dynamic_slice_in_dim(row_factor, own_col * TILE, TILE, 2)
    is_factor_col = (col_tiles < pivot_tiles)[None, None, :, None]
    trailing = jnp.where(is_factor_col, row_factor_cols[:, :, None, :], trailing)
    diag_rows = lax.dynamic_slice_in_dim(lower_factor, row_index * TILE, TILE, 0)
    diag_tile = lax.dynamic_slice_in_dim(diag_rows, own_col * TILE, TILE, 1)
    local_ids = jnp.arange(TILE, dtype=jnp.int32)
    global_row = row_index * TILE + local_ids[:, None]
    global_col = own_col * TILE + local_ids[None, :]
    diag_tile = jnp.where(global_row >= global_col, diag_tile, 0.0)
    top = jnp.where(is_factor_col[0], diag_tile[:, None, :], 0.0)
    top = jnp.broadcast_to(top, working[0].shape)
    working = jnp.concatenate([top[None], trailing], axis=0)
    factored = working.reshape(front.shape)
    contribution = jnp.where((col_tiles >= pivot_tiles)[None, None, :, None], working, 0.0)
    contrib_count = tile_map.shape[1]
    entry_ids = jnp.arange(contrib_count, dtype=jnp.int32)
    own_map = lax.dynamic_index_in_dim(tile_map, leaf_index, 0, keepdims=False)
    row_match = (row_tiles - pivot_tiles)[:, None] == entry_ids[None, :]
    row_targets = jnp.sum(jnp.where(row_match, own_map[None, :], 0), axis=1)
    row_valid = row_tiles >= pivot_tiles
    owner_count = leaf_count * row_count
    destination = row_targets % owner_count
    parent_row_slot = row_targets // owner_count
    slot_ids = jnp.arange(row_slots, dtype=jnp.int32)
    same_before = (
        (destination[None, :] == destination[:, None])
        & row_valid[None, :]
        & (slot_ids[None, :] < slot_ids[:, None])
    )
    rank_in_dest = jnp.sum(same_before.astype(jnp.int32), axis=1)
    capacity = (col_slots + row_count - 1) // row_count
    owner_ids = jnp.arange(owner_count, dtype=jnp.int32)
    capacity_ids = jnp.arange(capacity, dtype=jnp.int32)
    selection = (
        row_valid[None, None, :]
        & (destination[None, None, :] == owner_ids[:, None, None])
        & (rank_in_dest[None, None, :] == capacity_ids[None, :, None])
    )
    flattened = contribution.reshape(row_slots, -1)
    send_buffer = jnp.einsum(
        "oka,ax->okx",
        selection.astype(jnp.float32),
        flattened,
        precision=HIGHEST,
        preferred_element_type=jnp.float32,
    )
    chosen_slot = jnp.sum(jnp.where(selection, parent_row_slot[None, None, :], 0), axis=2)
    send_slots = jnp.where(jnp.any(selection, axis=2), chosen_slot, -1)
    received, received_slots = (
        lax.all_to_all(send_buffer, ("leaf", "row"), split_axis=0, concat_axis=0, tiled=True),
        lax.all_to_all(send_slots, ("leaf", "row"), split_axis=0, concat_axis=0, tiled=True),
    )
    received = received.reshape(leaf_count, row_count, capacity, -1)
    received_slots = received_slots.reshape(leaf_count, row_count, capacity)
    parent_local = parent[:, 0, 0, :, :, 0, :]
    parent_rows = parent_local.shape[0]
    parent_cols = parent_local.shape[2]
    row_place = (
        received_slots[None] == jnp.arange(parent_rows, dtype=jnp.int32)[:, None, None, None]
    ).astype(jnp.float32)
    by_leaf = jnp.einsum(
        "slrk,lrkx->slx", row_place, received, precision=HIGHEST, preferred_element_type=jnp.float32
    )
    by_leaf = by_leaf.reshape(parent_rows, leaf_count, TILE, col_slots, TILE)
    col_match = (col_tiles - pivot_tiles)[:, None] == entry_ids[None, :]
    col_targets = jnp.sum(jnp.where(col_match[None], tile_map[:, None, :], 0), axis=2)
    col_valid = col_tiles >= pivot_tiles
    parent_slot_ids = jnp.arange(parent_cols, dtype=jnp.int32)
    col_place = (
        col_valid[None, None, :]
        & (col_targets[:, None, :] // col_count == parent_slot_ids[None, :, None])
    ).astype(jnp.float32)
    assembled = jnp.einsum(
        "sltbv,lub->stuv", by_leaf, col_place, precision=HIGHEST, preferred_element_type=jnp.float32
    )
    new_parent = (parent_local + assembled).reshape(parent.shape)
    return (factored, new_parent)


def solution(mesh):
    return jax.shard_map(
        per_device,
        mesh=mesh,
        in_specs=(
            P("leaf", None, "row", None, None, "col", None),
            P(None, "leaf", "row", None, None, "col", None),
            P(),
            P(),
        ),
        out_specs=(
            P("leaf", None, "row", None, None, "col", None),
            P(None, "leaf", "row", None, None, "col", None),
        ),
        check_vma=False,
    )
```

```python
import jax
import jax.numpy as jnp
from jax import lax
from jax.sharding import PartitionSpec as P
from jax.experimental import pallas as pl
from jax.experimental.pallas import tpu as pltpu

TILE = 128
PB = 512
PANELS = 2
NPIV = 1024


HIGHEST = lax.Precision.HIGHEST


def spread(value, axis, source):
    kept = jnp.where(lax.axis_index(axis) == source, value, 0).astype(value.dtype)
    return lax.psum(kept, axis)


def update_slots(working, next_rows, column_factor, slot_low, slot_high):
    product = jnp.einsum(
        "atp,bsp->atbs",
        next_rows,
        column_factor,
        precision=HIGHEST,
        preferred_element_type=jnp.float32,
    )
    return working.at[:, :, slot_low:slot_high, :].add(-product)


def _chol_inverse_kernel(a_ref, l_ref, x_ref, lt_scr):
    size = a_ref.shape[0]
    block = a_ref[...]
    current = 0.5 * (block + block.T)
    lanes = lax.broadcasted_iota(jnp.int32, (size, size), 1)
    subs = lax.broadcasted_iota(jnp.int32, (size, size), 0)
    inverse = jnp.where(lanes == subs, 1.0, 0.0).astype(jnp.float32)
    lt_scr[...] = jnp.zeros((size, size), jnp.float32)
    row_ids = lax.broadcasted_iota(jnp.int32, (1, size), 1)
    group = 8
    for phase in range(size // group):
        top = phase * group
        active = size - top
        col_ids = lax.broadcasted_iota(jnp.int32, (active, 1), 0) + top
        for t in range(group):
            j = top + t
            row = current[t : t + 1, :]
            root = jnp.sqrt(row[:, j : j + 1])
            scale = 1.0 / root
            l_row = jnp.where(row_ids > j, row * scale, 0.0)
            l_row = jnp.where(row_ids == j, root, l_row)
            l_col = jnp.where(col_ids > j, current[:, j : j + 1] * scale, 0.0)
            l_col = jnp.where(col_ids == j, root, l_col)
            current = current - l_col * l_row
            lt_scr[j : j + 1, :] = l_row
            x_row = inverse[t : t + 1, :] * scale
            x_ref[j : j + 1, :] = x_row
            strict = jnp.where(col_ids > j, l_col, 0.0)
            inverse = inverse - strict * x_row
        current = current[group:, :]
        inverse = inverse[group:, :]
    l_ref[...] = lt_scr[...].T


def chol_inverse(block):
    size = block.shape[0]
    shape = jax.ShapeDtypeStruct((size, size), jnp.float32)
    return pl.pallas_call(
        _chol_inverse_kernel,
        out_shape=(shape, shape),
        scratch_shapes=[pltpu.VMEM((size, size), jnp.float32)],
    )(block)


def tall_cholesky(diagonal_block, below_rows):
    size = diagonal_block.shape[0]
    remaining = diagonal_block
    diag_columns = []
    inverses = []
    for step in range(size // TILE):
        low = step * TILE
        left = size - low - TILE
        pivot = remaining[:TILE, :TILE]
        pivot_factor, pivot_inverse = chol_inverse(pivot)
        inverses.append(pivot_inverse)
        parts = [jnp.zeros((low, TILE), jnp.float32), pivot_factor]
        if left:
            solved = jnp.dot(
                remaining[TILE:, :TILE],
                pivot_inverse.T,
                precision=HIGHEST,
                preferred_element_type=jnp.float32,
            )
            parts.append(solved)
            update = jnp.dot(
                solved, solved.T, precision=HIGHEST, preferred_element_type=jnp.float32
            )
            remaining = remaining[TILE:, TILE:] - update
        diag_columns.append(jnp.concatenate(parts, axis=0))
    lower_factor = jnp.concatenate(diag_columns, axis=1)
    rest = below_rows
    below_columns = []
    for step in range(size // TILE):
        low = step * TILE
        solved = jnp.dot(
            rest[:, :TILE], inverses[step].T, precision=HIGHEST, preferred_element_type=jnp.float32
        )
        below_columns.append(solved)
        if low + TILE < size:
            update = jnp.dot(
                solved,
                lower_factor[low + TILE :, low : low + TILE].T,
                precision=HIGHEST,
                preferred_element_type=jnp.float32,
            )
            rest = rest[:, TILE:] - update
    return lower_factor, jnp.concatenate(below_columns, axis=1)

def per_device(front, parent, tile_map, col_shift):
    leaf_count = lax.axis_size("leaf")
    row_count = lax.axis_size("row")
    col_count = lax.axis_size("col")
    leaf_index = lax.axis_index("leaf")
    row_index = lax.axis_index("row")
    col_index = lax.axis_index("col")
    local_front = front[0, :, 0, :, :, 0, :]
    row_slots = local_front.shape[0]
    col_slots = local_front.shape[2]
    pivot_tiles = NPIV // TILE
    assert pivot_tiles == row_count and pivot_tiles <= col_count
    row_tiles = jnp.arange(row_slots, dtype=jnp.int32) * row_count + row_index
    col_tiles = jnp.arange(col_slots, dtype=jnp.int32) * col_count + col_index

    working = local_front
    first_tiles = lax.all_gather(working[0, :, 0, :], "col", axis=0, tiled=False)
    diag_row = first_tiles[:pivot_tiles].transpose(1, 0, 2).reshape(TILE, NPIV)
    diagonal_block = lax.all_gather(diag_row, "row", axis=0, tiled=True)
    rest_cols, top_input, diagonal_block = lax.optimization_barrier(
        (working[1:, :, 0, :], working[0], diagonal_block)
    )
    first_cols = lax.all_gather(rest_cols, "col", axis=0, tiled=False)
    row_panel = first_cols[:pivot_tiles].transpose(1, 2, 0, 3).reshape(row_slots - 1, TILE, NPIV)
    top_rows = lax.all_gather(top_input, "row", axis=0, tiled=False)
    column_panel = top_rows.transpose(2, 3, 0, 1).reshape(col_slots, TILE, NPIV)
    stacked = jnp.concatenate(
        [row_panel.reshape(-1, NPIV), column_panel.reshape(-1, NPIV)], axis=0
    )
    lower_factor, solved = tall_cholesky(diagonal_block, stacked)
    trailing_rows = (row_slots - 1) * TILE
    row_factor = solved[:trailing_rows].reshape(row_slots - 1, TILE, NPIV)
    column_factor = solved[trailing_rows:].reshape(col_slots, TILE, NPIV)
    column_factor = jnp.where(
        (col_tiles >= pivot_tiles)[:, None, None], column_factor, 0.0
    )
    product = jnp.einsum(
        "atk,bsk->atbs",
        row_factor,
        column_factor,
        precision=HIGHEST,
        preferred_element_type=jnp.float32,
    )
    trailing = working[1:] - product
    own_col = jnp.minimum(col_index, pivot_tiles - 1)
    row_factor_cols = lax.dynamic_slice_in_dim(row_factor, own_col * TILE, TILE, 2)
    is_factor_col = (col_tiles < pivot_tiles)[None, None, :, None]
    trailing = jnp.where(is_factor_col, row_factor_cols[:, :, None, :], trailing)
    diag_rows = lax.dynamic_slice_in_dim(lower_factor, row_index * TILE, TILE, 0)
    diag_tile = lax.dynamic_slice_in_dim(diag_rows, own_col * TILE, TILE, 1)
    local_ids = jnp.arange(TILE, dtype=jnp.int32)
    global_row = row_index * TILE + local_ids[:, None]
    global_col = own_col * TILE + local_ids[None, :]
    diag_tile = jnp.where(global_row >= global_col, diag_tile, 0.0)
    top = jnp.where(is_factor_col[0], diag_tile[:, None, :], 0.0)
    top = jnp.broadcast_to(top, working[0].shape)
    working = jnp.concatenate([top[None], trailing], axis=0)
    factored = working.reshape(front.shape)
    contribution = jnp.where((col_tiles >= pivot_tiles)[None, None, :, None], working, 0.0)
    contrib_count = tile_map.shape[1]
    entry_ids = jnp.arange(contrib_count, dtype=jnp.int32)
    own_map = lax.dynamic_index_in_dim(tile_map, leaf_index, 0, keepdims=False)
    row_match = (row_tiles - pivot_tiles)[:, None] == entry_ids[None, :]
    row_targets = jnp.sum(jnp.where(row_match, own_map[None, :], 0), axis=1)
    row_valid = row_tiles >= pivot_tiles
    owner_count = leaf_count * row_count
    destination = row_targets % owner_count
    parent_row_slot = row_targets // owner_count
    slot_ids = jnp.arange(row_slots, dtype=jnp.int32)
    same_before = (
        (destination[None, :] == destination[:, None])
        & row_valid[None, :]
        & (slot_ids[None, :] < slot_ids[:, None])
    )
    rank_in_dest = jnp.sum(same_before.astype(jnp.int32), axis=1)
    capacity = (col_slots + row_count - 1) // row_count
    owner_ids = jnp.arange(owner_count, dtype=jnp.int32)
    capacity_ids = jnp.arange(capacity, dtype=jnp.int32)
    selection = (
        row_valid[None, None, :]
        & (destination[None, None, :] == owner_ids[:, None, None])
        & (rank_in_dest[None, None, :] == capacity_ids[None, :, None])
    )
    flattened = contribution.reshape(row_slots, -1)
    send_buffer = jnp.einsum(
        "oka,ax->okx",
        selection.astype(jnp.float32),
        flattened,
        precision=HIGHEST,
        preferred_element_type=jnp.float32,
    )
    chosen_slot = jnp.sum(jnp.where(selection, parent_row_slot[None, None, :], 0), axis=2)
    send_slots = jnp.where(jnp.any(selection, axis=2), chosen_slot, -1)
    received, received_slots = (
        lax.all_to_all(send_buffer, ("leaf", "row"), split_axis=0, concat_axis=0, tiled=True),
        lax.all_to_all(send_slots, ("leaf", "row"), split_axis=0, concat_axis=0, tiled=True),
    )
    received = received.reshape(leaf_count, row_count, capacity, -1)
    received_slots = received_slots.reshape(leaf_count, row_count, capacity)
    parent_local = parent[:, 0, 0, :, :, 0, :]
    parent_rows = parent_local.shape[0]
    parent_cols = parent_local.shape[2]
    row_place = (
        received_slots[None] == jnp.arange(parent_rows, dtype=jnp.int32)[:, None, None, None]
    ).astype(jnp.float32)
    by_leaf = jnp.einsum(
        "slrk,lrkx->slx", row_place, received, precision=HIGHEST, preferred_element_type=jnp.float32
    )
    by_leaf = by_leaf.reshape(parent_rows, leaf_count, TILE, col_slots, TILE)
    col_match = (col_tiles - pivot_tiles)[:, None] == entry_ids[None, :]
    col_targets = jnp.sum(jnp.where(col_match[None], tile_map[:, None, :], 0), axis=2)
    col_valid = col_tiles >= pivot_tiles
    parent_slot_ids = jnp.arange(parent_cols, dtype=jnp.int32)
    col_place = (
        col_valid[None, None, :]
        & (col_targets[:, None, :] // col_count == parent_slot_ids[None, :, None])
    ).astype(jnp.float32)
    assembled = jnp.einsum(
        "sltbv,lub->stuv", by_leaf, col_place, precision=HIGHEST, preferred_element_type=jnp.float32
    )
    new_parent = (parent_local + assembled).reshape(parent.shape)
    return (factored, new_parent)


def solution(mesh):
    return jax.shard_map(
        per_device,
        mesh=mesh,
        in_specs=(
            P("leaf", None, "row", None, None, "col", None),
            P(None, "leaf", "row", None, None, "col", None),
            P(),
            P(),
        ),
        out_specs=(
            P("leaf", None, "row", None, None, "col", None),
            P(None, "leaf", "row", None, None, "col", None),
        ),
        check_vma=False,
    )
```

```python
import jax
import jax.numpy as jnp
from jax import lax
from jax.sharding import PartitionSpec as P
from jax.experimental import pallas as pl
from jax.experimental.pallas import tpu as pltpu

TILE = 128
PB = 512
PANELS = 2
NPIV = 1024


HIGHEST = lax.Precision.HIGHEST
HIGH = lax.Precision.HIGH


def spread(value, axis, source):
    kept = jnp.where(lax.axis_index(axis) == source, value, 0).astype(value.dtype)
    return lax.psum(kept, axis)


def update_slots(working, next_rows, column_factor, slot_low, slot_high):
    product = jnp.einsum(
        "atp,bsp->atbs",
        next_rows,
        column_factor,
        precision=HIGHEST,
        preferred_element_type=jnp.float32,
    )
    return working.at[:, :, slot_low:slot_high, :].add(-product)


def _chol_inverse_kernel(a_ref, l_ref, x_ref, lt_scr):
    size = a_ref.shape[0]
    block = a_ref[...]
    current = 0.5 * (block + block.T)
    lanes = lax.broadcasted_iota(jnp.int32, (size, size), 1)
    subs = lax.broadcasted_iota(jnp.int32, (size, size), 0)
    inverse = jnp.where(lanes == subs, 1.0, 0.0).astype(jnp.float32)
    lt_scr[...] = jnp.zeros((size, size), jnp.float32)
    row_ids = lax.broadcasted_iota(jnp.int32, (1, size), 1)
    group = 8
    for phase in range(size // group):
        top = phase * group
        active = size - top
        col_ids = lax.broadcasted_iota(jnp.int32, (active, 1), 0) + top
        for t in range(group):
            j = top + t
            row = current[t : t + 1, :]
            pivot = row[:, j : j + 1]
            root = jnp.sqrt(pivot)
            scale = lax.rsqrt(pivot)
            l_row = jnp.where(row_ids > j, row * scale, 0.0)
            l_row = jnp.where(row_ids == j, root, l_row)
            l_col = jnp.where(col_ids > j, current[:, j : j + 1] * scale, 0.0)
            l_col = jnp.where(col_ids == j, root, l_col)
            current = current - l_col * l_row
            lt_scr[j : j + 1, :] = l_row
            x_row = inverse[t : t + 1, :] * scale
            x_ref[j : j + 1, :] = x_row
            strict = jnp.where(col_ids > j, l_col, 0.0)
            inverse = inverse - strict * x_row
        current = current[group:, :]
        inverse = inverse[group:, :]
    l_ref[...] = lt_scr[...].T


def chol_inverse(block):
    size = block.shape[0]
    shape = jax.ShapeDtypeStruct((size, size), jnp.float32)
    return pl.pallas_call(
        _chol_inverse_kernel,
        out_shape=(shape, shape),
        scratch_shapes=[pltpu.VMEM((size, size), jnp.float32)],
    )(block)


def tall_cholesky(diagonal_block, below_rows):
    size = diagonal_block.shape[0]
    remaining = diagonal_block
    diag_columns = []
    inverses = []
    for step in range(size // TILE):
        low = step * TILE
        left = size - low - TILE
        pivot = remaining[:TILE, :TILE]
        pivot_factor, pivot_inverse = chol_inverse(pivot)
        inverses.append(pivot_inverse)
        parts = [jnp.zeros((low, TILE), jnp.float32), pivot_factor]
        if left:
            solved = jnp.dot(
                remaining[TILE:, :TILE],
                pivot_inverse.T,
                precision=HIGHEST,
                preferred_element_type=jnp.float32,
            )
            parts.append(solved)
            update = jnp.dot(
                solved, solved.T, precision=HIGHEST, preferred_element_type=jnp.float32
            )
            remaining = remaining[TILE:, TILE:] - update
        diag_columns.append(jnp.concatenate(parts, axis=0))
    lower_factor = jnp.concatenate(diag_columns, axis=1)
    rest = below_rows
    below_columns = []
    for step in range(size // TILE):
        low = step * TILE
        solved = jnp.dot(
            rest[:, :TILE], inverses[step].T, precision=HIGH, preferred_element_type=jnp.float32
        )
        below_columns.append(solved)
        if low + TILE < size:
            update = jnp.dot(
                solved,
                lower_factor[low + TILE :, low : low + TILE].T,
                precision=HIGH,
                preferred_element_type=jnp.float32,
            )
            rest = rest[:, TILE:] - update
    return lower_factor, jnp.concatenate(below_columns, axis=1)

def per_device(front, parent, tile_map, col_shift):
    leaf_count = lax.axis_size("leaf")
    row_count = lax.axis_size("row")
    col_count = lax.axis_size("col")
    leaf_index = lax.axis_index("leaf")
    row_index = lax.axis_index("row")
    col_index = lax.axis_index("col")
    local_front = front[0, :, 0, :, :, 0, :]
    row_slots = local_front.shape[0]
    col_slots = local_front.shape[2]
    pivot_tiles = NPIV // TILE
    assert pivot_tiles == row_count and pivot_tiles <= col_count
    row_tiles = jnp.arange(row_slots, dtype=jnp.int32) * row_count + row_index
    col_tiles = jnp.arange(col_slots, dtype=jnp.int32) * col_count + col_index

    working = local_front
    first_tiles = lax.all_gather(working[0, :, 0, :], "col", axis=0, tiled=False)
    diag_row = first_tiles[:pivot_tiles].transpose(1, 0, 2).reshape(TILE, NPIV)
    diagonal_block = lax.all_gather(diag_row, "row", axis=0, tiled=True)
    rest_cols, top_input, diagonal_block = lax.optimization_barrier(
        (working[1:, :, 0, :], working[0], diagonal_block)
    )
    first_cols = lax.all_gather(rest_cols, "col", axis=0, tiled=False)
    row_panel = first_cols[:pivot_tiles].transpose(1, 2, 0, 3).reshape(row_slots - 1, TILE, NPIV)
    top_rows = lax.all_gather(top_input, "row", axis=0, tiled=False)
    column_panel = top_rows.transpose(2, 3, 0, 1).reshape(col_slots, TILE, NPIV)
    stacked = jnp.concatenate(
        [row_panel.reshape(-1, NPIV), column_panel.reshape(-1, NPIV)], axis=0
    )
    lower_factor, solved = tall_cholesky(diagonal_block, stacked)
    trailing_rows = (row_slots - 1) * TILE
    row_factor = solved[:trailing_rows].reshape(row_slots - 1, TILE, NPIV)
    column_factor = solved[trailing_rows:].reshape(col_slots, TILE, NPIV)
    column_factor = jnp.where(
        (col_tiles >= pivot_tiles)[:, None, None], column_factor, 0.0
    )
    product = jnp.einsum(
        "atk,bsk->atbs",
        row_factor,
        column_factor,
        precision=HIGH,
        preferred_element_type=jnp.float32,
    )
    trailing = working[1:] - product
    own_col = jnp.minimum(col_index, pivot_tiles - 1)
    row_factor_cols = lax.dynamic_slice_in_dim(row_factor, own_col * TILE, TILE, 2)
    is_factor_col = (col_tiles < pivot_tiles)[None, None, :, None]
    trailing = jnp.where(is_factor_col, row_factor_cols[:, :, None, :], trailing)
    diag_rows = lax.dynamic_slice_in_dim(lower_factor, row_index * TILE, TILE, 0)
    diag_tile = lax.dynamic_slice_in_dim(diag_rows, own_col * TILE, TILE, 1)
    local_ids = jnp.arange(TILE, dtype=jnp.int32)
    global_row = row_index * TILE + local_ids[:, None]
    global_col = own_col * TILE + local_ids[None, :]
    diag_tile = jnp.where(global_row >= global_col, diag_tile, 0.0)
    top = jnp.where(is_factor_col[0], diag_tile[:, None, :], 0.0)
    top = jnp.broadcast_to(top, working[0].shape)
    working = jnp.concatenate([top[None], trailing], axis=0)
    factored = working.reshape(front.shape)
    contribution = jnp.where((col_tiles >= pivot_tiles)[None, None, :, None], working, 0.0)
    contrib_count = tile_map.shape[1]
    entry_ids = jnp.arange(contrib_count, dtype=jnp.int32)
    own_map = lax.dynamic_index_in_dim(tile_map, leaf_index, 0, keepdims=False)
    row_match = (row_tiles - pivot_tiles)[:, None] == entry_ids[None, :]
    row_targets = jnp.sum(jnp.where(row_match, own_map[None, :], 0), axis=1)
    row_valid = row_tiles >= pivot_tiles
    owner_count = leaf_count * row_count
    destination = row_targets % owner_count
    parent_row_slot = row_targets // owner_count
    slot_ids = jnp.arange(row_slots, dtype=jnp.int32)
    same_before = (
        (destination[None, :] == destination[:, None])
        & row_valid[None, :]
        & (slot_ids[None, :] < slot_ids[:, None])
    )
    rank_in_dest = jnp.sum(same_before.astype(jnp.int32), axis=1)
    capacity = (col_slots + row_count - 1) // row_count
    owner_ids = jnp.arange(owner_count, dtype=jnp.int32)
    capacity_ids = jnp.arange(capacity, dtype=jnp.int32)
    selection = (
        row_valid[None, None, :]
        & (destination[None, None, :] == owner_ids[:, None, None])
        & (rank_in_dest[None, None, :] == capacity_ids[None, :, None])
    )
    flattened = contribution.reshape(row_slots, -1)
    send_buffer = jnp.einsum(
        "oka,ax->okx",
        selection.astype(jnp.float32),
        flattened,
        precision=HIGHEST,
        preferred_element_type=jnp.float32,
    )
    chosen_slot = jnp.sum(jnp.where(selection, parent_row_slot[None, None, :], 0), axis=2)
    send_slots = jnp.where(jnp.any(selection, axis=2), chosen_slot, -1)
    received, received_slots = (
        lax.all_to_all(send_buffer, ("leaf", "row"), split_axis=0, concat_axis=0, tiled=True),
        lax.all_to_all(send_slots, ("leaf", "row"), split_axis=0, concat_axis=0, tiled=True),
    )
    received = received.reshape(leaf_count, row_count, capacity, -1)
    received_slots = received_slots.reshape(leaf_count, row_count, capacity)
    parent_local = parent[:, 0, 0, :, :, 0, :]
    parent_rows = parent_local.shape[0]
    parent_cols = parent_local.shape[2]
    row_place = (
        received_slots[None] == jnp.arange(parent_rows, dtype=jnp.int32)[:, None, None, None]
    ).astype(jnp.float32)
    by_leaf = jnp.einsum(
        "slrk,lrkx->slx", row_place, received, precision=HIGHEST, preferred_element_type=jnp.float32
    )
    by_leaf = by_leaf.reshape(parent_rows, leaf_count, TILE, col_slots, TILE)
    col_match = (col_tiles - pivot_tiles)[:, None] == entry_ids[None, :]
    col_targets = jnp.sum(jnp.where(col_match[None], tile_map[:, None, :], 0), axis=2)
    col_valid = col_tiles >= pivot_tiles
    parent_slot_ids = jnp.arange(parent_cols, dtype=jnp.int32)
    col_place = (
        col_valid[None, None, :]
        & (col_targets[:, None, :] // col_count == parent_slot_ids[None, :, None])
    ).astype(jnp.float32)
    assembled = jnp.einsum(
        "sltbv,lub->stuv", by_leaf, col_place, precision=HIGHEST, preferred_element_type=jnp.float32
    )
    new_parent = (parent_local + assembled).reshape(parent.shape)
    return (factored, new_parent)


def solution(mesh):
    return jax.shard_map(
        per_device,
        mesh=mesh,
        in_specs=(
            P("leaf", None, "row", None, None, "col", None),
            P(None, "leaf", "row", None, None, "col", None),
            P(),
            P(),
        ),
        out_specs=(
            P("leaf", None, "row", None, None, "col", None),
            P(None, "leaf", "row", None, None, "col", None),
        ),
        check_vma=False,
    )
```

```python
import jax
import jax.numpy as jnp
from jax import lax
from jax.sharding import PartitionSpec as P
from jax.experimental import pallas as pl
from jax.experimental.pallas import tpu as pltpu

TILE = 128
PB = 512
PANELS = 2
NPIV = 1024


HIGHEST = lax.Precision.HIGHEST
HIGH = lax.Precision.HIGH


def spread(value, axis, source):
    kept = jnp.where(lax.axis_index(axis) == source, value, 0).astype(value.dtype)
    return lax.psum(kept, axis)


def update_slots(working, next_rows, column_factor, slot_low, slot_high):
    product = jnp.einsum(
        "atp,bsp->atbs",
        next_rows,
        column_factor,
        precision=HIGHEST,
        preferred_element_type=jnp.float32,
    )
    return working.at[:, :, slot_low:slot_high, :].add(-product)


def _chol_inverse_kernel(a_ref, l_ref, x_ref, lt_scr):
    size = a_ref.shape[0]
    block = a_ref[...]
    current = 0.5 * (block + block.T)
    lanes = lax.broadcasted_iota(jnp.int32, (size, size), 1)
    subs = lax.broadcasted_iota(jnp.int32, (size, size), 0)
    inverse = jnp.where(lanes == subs, 1.0, 0.0).astype(jnp.float32)
    lt_scr[...] = jnp.zeros((size, size), jnp.float32)
    row_ids = lax.broadcasted_iota(jnp.int32, (1, size), 1)
    group = 8
    for phase in range(size // group):
        top = phase * group
        active = size - top
        col_ids = lax.broadcasted_iota(jnp.int32, (active, 1), 0) + top
        for t in range(group):
            j = top + t
            row = current[t : t + 1, :]
            pivot = row[:, j : j + 1]
            root = jnp.sqrt(pivot)
            scale = lax.rsqrt(pivot)
            l_row = jnp.where(row_ids > j, row * scale, 0.0)
            l_row = jnp.where(row_ids == j, root, l_row)
            l_col = jnp.where(col_ids > j, current[:, j : j + 1] * scale, 0.0)
            l_col = jnp.where(col_ids == j, root, l_col)
            current = current - l_col * l_row
            lt_scr[j : j + 1, :] = l_row
            x_row = inverse[t : t + 1, :] * scale
            x_ref[j : j + 1, :] = x_row
            strict = jnp.where(col_ids > j, l_col, 0.0)
            inverse = inverse - strict * x_row
        current = current[group:, :]
        inverse = inverse[group:, :]
    l_ref[...] = lt_scr[...].T


def chol_inverse(block):
    size = block.shape[0]
    shape = jax.ShapeDtypeStruct((size, size), jnp.float32)
    return pl.pallas_call(
        _chol_inverse_kernel,
        out_shape=(shape, shape),
        scratch_shapes=[pltpu.VMEM((size, size), jnp.float32)],
    )(block)


def tall_cholesky(diagonal_block, below_rows):
    size = diagonal_block.shape[0]
    remaining = diagonal_block
    diag_columns = []
    inverses = []
    for step in range(size // TILE):
        low = step * TILE
        left = size - low - TILE
        pivot = remaining[:TILE, :TILE]
        pivot_factor, pivot_inverse = chol_inverse(pivot)
        inverses.append(pivot_inverse)
        parts = [jnp.zeros((low, TILE), jnp.float32), pivot_factor]
        if left:
            solved = jnp.dot(
                remaining[TILE:, :TILE],
                pivot_inverse.T,
                precision=HIGHEST,
                preferred_element_type=jnp.float32,
            )
            parts.append(solved)
            update = jnp.dot(
                solved, solved.T, precision=HIGHEST, preferred_element_type=jnp.float32
            )
            remaining = remaining[TILE:, TILE:] - update
        diag_columns.append(jnp.concatenate(parts, axis=0))
    lower_factor = jnp.concatenate(diag_columns, axis=1)
    rest = below_rows
    below_columns = []
    for step in range(size // TILE):
        low = step * TILE
        solved = jnp.dot(
            rest[:, :TILE], inverses[step].T, precision=HIGH, preferred_element_type=jnp.float32
        )
        below_columns.append(solved)
        if low + TILE < size:
            update = jnp.dot(
                solved,
                lower_factor[low + TILE :, low : low + TILE].T,
                precision=HIGH,
                preferred_element_type=jnp.float32,
            )
            rest = rest[:, TILE:] - update
    return lower_factor, jnp.concatenate(below_columns, axis=1)

def per_device(front, parent, tile_map, col_shift):
    leaf_count = lax.axis_size("leaf")
    row_count = lax.axis_size("row")
    col_count = lax.axis_size("col")
    leaf_index = lax.axis_index("leaf")
    row_index = lax.axis_index("row")
    col_index = lax.axis_index("col")
    local_front = front[0, :, 0, :, :, 0, :]
    row_slots = local_front.shape[0]
    col_slots = local_front.shape[2]
    pivot_tiles = NPIV // TILE
    assert pivot_tiles == row_count and pivot_tiles <= col_count
    row_tiles = jnp.arange(row_slots, dtype=jnp.int32) * row_count + row_index
    col_tiles = jnp.arange(col_slots, dtype=jnp.int32) * col_count + col_index

    working = local_front
    first_tiles = lax.all_gather(working[0, :, 0, :], "col", axis=0, tiled=False)
    diag_row = first_tiles[:pivot_tiles].transpose(1, 0, 2).reshape(TILE, NPIV)
    diagonal_block = lax.all_gather(diag_row, "row", axis=0, tiled=True)
    rest_cols, top_input, diagonal_block = lax.optimization_barrier(
        (working[1:, :, 0, :], working[0], diagonal_block)
    )
    first_cols = lax.all_gather(rest_cols, "col", axis=0, tiled=False)
    row_panel = first_cols[:pivot_tiles].transpose(1, 2, 0, 3).reshape(row_slots - 1, TILE, NPIV)
    top_rows = lax.all_gather(top_input, "row", axis=0, tiled=False)
    column_panel = top_rows.transpose(2, 3, 0, 1).reshape(col_slots, TILE, NPIV)
    stacked = jnp.concatenate(
        [row_panel.reshape(-1, NPIV), column_panel.reshape(-1, NPIV)], axis=0
    )
    lower_factor, solved = tall_cholesky(diagonal_block, stacked)
    trailing_rows = (row_slots - 1) * TILE
    row_factor = solved[:trailing_rows].reshape(row_slots - 1, TILE, NPIV)
    column_factor = solved[trailing_rows:].reshape(col_slots, TILE, NPIV)
    column_factor = jnp.where(
        (col_tiles >= pivot_tiles)[:, None, None], column_factor, 0.0
    )
    product = jnp.einsum(
        "atk,bsk->atbs",
        row_factor,
        column_factor,
        precision=HIGH,
        preferred_element_type=jnp.float32,
    )
    trailing = working[1:] - product
    own_col = jnp.minimum(col_index, pivot_tiles - 1)
    row_factor_cols = lax.dynamic_slice_in_dim(row_factor, own_col * TILE, TILE, 2)
    is_factor_col = (col_tiles < pivot_tiles)[None, None, :, None]
    trailing = jnp.where(is_factor_col, row_factor_cols[:, :, None, :], trailing)
    diag_rows = lax.dynamic_slice_in_dim(lower_factor, row_index * TILE, TILE, 0)
    diag_tile = lax.dynamic_slice_in_dim(diag_rows, own_col * TILE, TILE, 1)
    local_ids = jnp.arange(TILE, dtype=jnp.int32)
    global_row = row_index * TILE + local_ids[:, None]
    global_col = own_col * TILE + local_ids[None, :]
    diag_tile = jnp.where(global_row >= global_col, diag_tile, 0.0)
    top = jnp.where(is_factor_col[0], diag_tile[:, None, :], 0.0)
    top = jnp.broadcast_to(top, working[0].shape)
    working = jnp.concatenate([top[None], trailing], axis=0)
    factored = working.reshape(front.shape)
    contribution = jnp.where((col_tiles >= pivot_tiles)[None, None, :, None], working, 0.0)
    contrib_count = tile_map.shape[1]
    entry_ids = jnp.arange(contrib_count, dtype=jnp.int32)
    own_map = lax.dynamic_index_in_dim(tile_map, leaf_index, 0, keepdims=False)
    row_match = (row_tiles - pivot_tiles)[:, None] == entry_ids[None, :]
    row_targets = jnp.sum(jnp.where(row_match, own_map[None, :], 0), axis=1)
    row_valid = row_tiles >= pivot_tiles
    owner_count = leaf_count * row_count
    destination = row_targets % owner_count
    parent_row_slot = row_targets // owner_count
    owner_ids = jnp.arange(owner_count, dtype=jnp.int32)
    slot_ids = jnp.arange(row_slots, dtype=jnp.int32)
    selection = row_valid[None, :] & (destination[None, :] == owner_ids[:, None])
    source_slot = jnp.sum(jnp.where(selection, slot_ids[None, :], 0), axis=1)
    has_source = jnp.any(selection, axis=1)
    send_slots = jnp.where(
        has_source, jnp.sum(jnp.where(selection, parent_row_slot[None, :], 0), axis=1), -1
    )
    pieces = [
        lax.dynamic_index_in_dim(contribution, source_slot[o], 0, keepdims=False)
        for o in range(owner_count)
    ]
    send_buffer = jnp.where(has_source[:, None, None, None], jnp.stack(pieces), 0.0)
    received, received_slots = (
        lax.all_to_all(send_buffer, ("leaf", "row"), split_axis=0, concat_axis=0, tiled=True),
        lax.all_to_all(send_slots, ("leaf", "row"), split_axis=0, concat_axis=0, tiled=True),
    )
    parent_local = parent[:, 0, 0, :, :, 0, :]
    parent_rows = parent_local.shape[0]
    parent_cols = parent_local.shape[2]
    received_slots = received_slots.reshape(leaf_count, row_count)
    row_ids = jnp.arange(row_count, dtype=jnp.int32)
    col_valid = col_tiles >= pivot_tiles
    col_match = (col_tiles - pivot_tiles)[:, None] == entry_ids[None, :]
    col_targets = jnp.sum(jnp.where(col_match[None], tile_map[:, None, :], 0), axis=2)
    col_ids = jnp.arange(col_slots, dtype=jnp.int32)
    assembled = jnp.zeros(parent_local.shape, jnp.float32)
    for leaf in range(leaf_count):
        row_hit = received_slots[leaf][None, :] == jnp.arange(parent_rows, dtype=jnp.int32)[:, None]
        from_row = jnp.sum(jnp.where(row_hit, row_ids[None, :], 0), axis=1)
        row_any = jnp.any(row_hit, axis=1)
        col_hit = col_valid[None, :] & (
            col_targets[leaf][None, :] // col_count
            == jnp.arange(parent_cols, dtype=jnp.int32)[:, None]
        )
        from_col = jnp.sum(jnp.where(col_hit, col_ids[None, :], 0), axis=1)
        col_any = jnp.any(col_hit, axis=1)
        rows_of_leaf = jnp.stack(
            [
                lax.dynamic_index_in_dim(received, leaf * row_count + from_row[p], 0, keepdims=False)
                for p in range(parent_rows)
            ]
        )
        placed = jnp.stack(
            [
                lax.dynamic_index_in_dim(rows_of_leaf, from_col[u], 2, keepdims=False)
                for u in range(parent_cols)
            ],
            axis=2,
        )
        keep = row_any[:, None, None, None] & col_any[None, None, :, None]
        assembled = assembled + jnp.where(keep, placed, 0.0)
    new_parent = (parent_local + assembled).reshape(parent.shape)
    return (factored, new_parent)


def solution(mesh):
    return jax.shard_map(
        per_device,
        mesh=mesh,
        in_specs=(
            P("leaf", None, "row", None, None, "col", None),
            P(None, "leaf", "row", None, None, "col", None),
            P(),
            P(),
        ),
        out_specs=(
            P("leaf", None, "row", None, None, "col", None),
            P(None, "leaf", "row", None, None, "col", None),
        ),
        check_vma=False,
    )
```

```python
import jax
import jax.numpy as jnp
from jax import lax
from jax.sharding import PartitionSpec as P
from jax.experimental import pallas as pl
from jax.experimental.pallas import tpu as pltpu

TILE = 128
PB = 512
PANELS = 2
NPIV = 1024


HIGHEST = lax.Precision.HIGHEST
HIGH = lax.Precision.HIGH


def spread(value, axis, source):
    kept = jnp.where(lax.axis_index(axis) == source, value, 0).astype(value.dtype)
    return lax.psum(kept, axis)


def update_slots(working, next_rows, column_factor, slot_low, slot_high):
    product = jnp.einsum(
        "atp,bsp->atbs",
        next_rows,
        column_factor,
        precision=HIGHEST,
        preferred_element_type=jnp.float32,
    )
    return working.at[:, :, slot_low:slot_high, :].add(-product)


def _chol_inverse_kernel(a_ref, l_ref, x_ref, lt_scr):
    size = a_ref.shape[0]
    block = a_ref[...]
    current = 0.5 * (block + block.T)
    lanes = lax.broadcasted_iota(jnp.int32, (size, size), 1)
    subs = lax.broadcasted_iota(jnp.int32, (size, size), 0)
    inverse = jnp.where(lanes == subs, 1.0, 0.0).astype(jnp.float32)
    lt_scr[...] = jnp.zeros((size, size), jnp.float32)
    row_ids = lax.broadcasted_iota(jnp.int32, (1, size), 1)
    group = 8
    for phase in range(size // group):
        top = phase * group
        active = size - top
        col_ids = lax.broadcasted_iota(jnp.int32, (active, 1), 0) + top
        for t in range(group):
            j = top + t
            row = current[t : t + 1, :]
            pivot = row[:, j : j + 1]
            root = jnp.sqrt(pivot)
            scale = lax.rsqrt(pivot)
            l_row = jnp.where(row_ids > j, row * scale, 0.0)
            l_row = jnp.where(row_ids == j, root, l_row)
            l_col = jnp.where(col_ids > j, current[:, j : j + 1] * scale, 0.0)
            l_col = jnp.where(col_ids == j, root, l_col)
            current = current - l_col * l_row
            lt_scr[j : j + 1, :] = l_row
            x_row = inverse[t : t + 1, :] * scale
            x_ref[j : j + 1, :] = x_row
            strict = jnp.where(col_ids > j, l_col, 0.0)
            inverse = inverse - strict * x_row
        current = current[group:, :]
        inverse = inverse[group:, :]
    l_ref[...] = lt_scr[...].T


def chol_inverse(block):
    size = block.shape[0]
    shape = jax.ShapeDtypeStruct((size, size), jnp.float32)
    return pl.pallas_call(
        _chol_inverse_kernel,
        out_shape=(shape, shape),
        scratch_shapes=[pltpu.VMEM((size, size), jnp.float32)],
    )(block)


def tall_cholesky(diagonal_block, below_rows):
    size = diagonal_block.shape[0]
    remaining = diagonal_block
    diag_columns = []
    inverses = []
    for step in range(size // TILE):
        low = step * TILE
        left = size - low - TILE
        pivot = remaining[:TILE, :TILE]
        pivot_factor, pivot_inverse = chol_inverse(pivot)
        inverses.append(pivot_inverse)
        parts = [jnp.zeros((low, TILE), jnp.float32), pivot_factor]
        if left:
            solved = jnp.dot(
                remaining[TILE:, :TILE],
                pivot_inverse.T,
                precision=HIGHEST,
                preferred_element_type=jnp.float32,
            )
            parts.append(solved)
            update = jnp.dot(
                solved, solved.T, precision=HIGHEST, preferred_element_type=jnp.float32
            )
            remaining = remaining[TILE:, TILE:] - update
        diag_columns.append(jnp.concatenate(parts, axis=0))
    lower_factor = jnp.concatenate(diag_columns, axis=1)
    rest = below_rows
    below_columns = []
    for step in range(size // TILE):
        low = step * TILE
        solved = jnp.dot(
            rest[:, :TILE], inverses[step].T, precision=HIGH, preferred_element_type=jnp.float32
        )
        below_columns.append(solved)
        if low + TILE < size:
            update = jnp.dot(
                solved,
                lower_factor[low + TILE :, low : low + TILE].T,
                precision=HIGH,
                preferred_element_type=jnp.float32,
            )
            rest = rest[:, TILE:] - update
    return lower_factor, jnp.concatenate(below_columns, axis=1)

def per_device(front, parent, tile_map, col_shift):
    leaf_count = lax.axis_size("leaf")
    row_count = lax.axis_size("row")
    col_count = lax.axis_size("col")
    leaf_index = lax.axis_index("leaf")
    row_index = lax.axis_index("row")
    col_index = lax.axis_index("col")
    local_front = front[0, :, 0, :, :, 0, :]
    row_slots = local_front.shape[0]
    col_slots = local_front.shape[2]
    pivot_tiles = NPIV // TILE
    assert pivot_tiles == row_count and pivot_tiles <= col_count
    row_tiles = jnp.arange(row_slots, dtype=jnp.int32) * row_count + row_index
    col_tiles = jnp.arange(col_slots, dtype=jnp.int32) * col_count + col_index

    working = local_front
    first_tiles = lax.all_gather(working[0, :, 0, :], "col", axis=0, tiled=False)
    diag_row = first_tiles[:pivot_tiles].transpose(1, 0, 2).reshape(TILE, NPIV)
    diagonal_block = lax.all_gather(diag_row, "row", axis=0, tiled=True)
    rest_cols, top_input, diagonal_block = lax.optimization_barrier(
        (working[1:, :, 0, :], working[0], diagonal_block)
    )
    first_cols = lax.all_gather(rest_cols, "col", axis=0, tiled=False)
    row_panel = first_cols[:pivot_tiles].transpose(1, 2, 0, 3).reshape(row_slots - 1, TILE, NPIV)
    top_rows = lax.all_gather(top_input, "row", axis=0, tiled=False)
    column_panel = top_rows.transpose(2, 3, 0, 1).reshape(col_slots, TILE, NPIV)
    stacked = jnp.concatenate(
        [row_panel.reshape(-1, NPIV), column_panel.reshape(-1, NPIV)], axis=0
    )
    lower_factor, solved = tall_cholesky(diagonal_block, stacked)
    trailing_rows = (row_slots - 1) * TILE
    row_factor = solved[:trailing_rows].reshape(row_slots - 1, TILE, NPIV)
    column_factor = solved[trailing_rows:].reshape(col_slots, TILE, NPIV)
    column_factor = jnp.where(
        (col_tiles >= pivot_tiles)[:, None, None], column_factor, 0.0
    )
    product = jnp.einsum(
        "atk,bsk->atbs",
        row_factor,
        column_factor,
        precision=HIGH,
        preferred_element_type=jnp.float32,
    )
    trailing = working[1:] - product
    own_col = jnp.minimum(col_index, pivot_tiles - 1)
    row_factor_cols = lax.dynamic_slice_in_dim(row_factor, own_col * TILE, TILE, 2)
    is_factor_col = (col_tiles < pivot_tiles)[None, None, :, None]
    trailing = jnp.where(is_factor_col, row_factor_cols[:, :, None, :], trailing)
    diag_rows = lax.dynamic_slice_in_dim(lower_factor, row_index * TILE, TILE, 0)
    diag_tile = lax.dynamic_slice_in_dim(diag_rows, own_col * TILE, TILE, 1)
    local_ids = jnp.arange(TILE, dtype=jnp.int32)
    global_row = row_index * TILE + local_ids[:, None]
    global_col = own_col * TILE + local_ids[None, :]
    diag_tile = jnp.where(global_row >= global_col, diag_tile, 0.0)
    top = jnp.where(is_factor_col[0], diag_tile[:, None, :], 0.0)
    top = jnp.broadcast_to(top, working[0].shape)
    working = jnp.concatenate([top[None], trailing], axis=0)
    factored = working.reshape(front.shape)
    contribution = jnp.where((col_tiles >= pivot_tiles)[None, None, :, None], working, 0.0)
    contrib_count = tile_map.shape[1]
    entry_ids = jnp.arange(contrib_count, dtype=jnp.int32)
    own_map = lax.dynamic_index_in_dim(tile_map, leaf_index, 0, keepdims=False)
    row_match = (row_tiles - pivot_tiles)[:, None] == entry_ids[None, :]
    row_targets = jnp.sum(jnp.where(row_match, own_map[None, :], 0), axis=1)
    row_valid = row_tiles >= pivot_tiles
    owner_count = leaf_count * row_count
    destination = row_targets % owner_count
    parent_row_slot = row_targets // owner_count
    owner_ids = jnp.arange(owner_count, dtype=jnp.int32)
    slot_ids = jnp.arange(row_slots, dtype=jnp.int32)
    selection = row_valid[None, :] & (destination[None, :] == owner_ids[:, None])
    source_slot = jnp.sum(jnp.where(selection, slot_ids[None, :], 0), axis=1)
    has_source = jnp.any(selection, axis=1)
    pieces = [
        lax.dynamic_index_in_dim(contribution, source_slot[o], 0, keepdims=False)
        for o in range(owner_count)
    ]
    send_buffer = jnp.where(has_source[:, None, None, None], jnp.stack(pieces), 0.0)
    received = lax.all_to_all(
        send_buffer, ("leaf", "row"), split_axis=0, concat_axis=0, tiled=True
    )
    parent_local = parent[:, 0, 0, :, :, 0, :]
    parent_rows = parent_local.shape[0]
    parent_cols = parent_local.shape[2]
    my_owner = leaf_index * row_count + row_index
    by_source = tile_map.reshape(leaf_count, contrib_count // row_count, row_count)
    source_hit = by_source % owner_count == my_owner
    received_slots = jnp.where(
        jnp.any(source_hit, axis=1),
        jnp.sum(jnp.where(source_hit, by_source // owner_count, 0), axis=1),
        -1,
    )
    row_ids = jnp.arange(row_count, dtype=jnp.int32)
    col_valid = col_tiles >= pivot_tiles
    col_match = (col_tiles - pivot_tiles)[:, None] == entry_ids[None, :]
    col_targets = jnp.sum(jnp.where(col_match[None], tile_map[:, None, :], 0), axis=2)
    col_ids = jnp.arange(col_slots, dtype=jnp.int32)
    assembled = jnp.zeros(parent_local.shape, jnp.float32)
    for leaf in range(leaf_count):
        row_hit = received_slots[leaf][None, :] == jnp.arange(parent_rows, dtype=jnp.int32)[:, None]
        from_row = jnp.sum(jnp.where(row_hit, row_ids[None, :], 0), axis=1)
        row_any = jnp.any(row_hit, axis=1)
        col_hit = col_valid[None, :] & (
            col_targets[leaf][None, :] // col_count
            == jnp.arange(parent_cols, dtype=jnp.int32)[:, None]
        )
        from_col = jnp.sum(jnp.where(col_hit, col_ids[None, :], 0), axis=1)
        col_any = jnp.any(col_hit, axis=1)
        rows_of_leaf = jnp.stack(
            [
                lax.dynamic_index_in_dim(received, leaf * row_count + from_row[p], 0, keepdims=False)
                for p in range(parent_rows)
            ]
        )
        placed = jnp.stack(
            [
                lax.dynamic_index_in_dim(rows_of_leaf, from_col[u], 2, keepdims=False)
                for u in range(parent_cols)
            ],
            axis=2,
        )
        keep = row_any[:, None, None, None] & col_any[None, None, :, None]
        assembled = assembled + jnp.where(keep, placed, 0.0)
    new_parent = (parent_local + assembled).reshape(parent.shape)
    return (factored, new_parent)


def solution(mesh):
    return jax.shard_map(
        per_device,
        mesh=mesh,
        in_specs=(
            P("leaf", None, "row", None, None, "col", None),
            P(None, "leaf", "row", None, None, "col", None),
            P(),
            P(),
        ),
        out_specs=(
            P("leaf", None, "row", None, None, "col", None),
            P(None, "leaf", "row", None, None, "col", None),
        ),
        check_vma=False,
    )
```

```python
import jax
import jax.numpy as jnp
from jax import lax
from jax.sharding import PartitionSpec as P
from jax.experimental import pallas as pl
from jax.experimental.pallas import tpu as pltpu

TILE = 128
PB = 512
PANELS = 2
NPIV = 1024


HIGHEST = lax.Precision.HIGHEST
HIGH = lax.Precision.HIGH


def spread(value, axis, source):
    kept = jnp.where(lax.axis_index(axis) == source, value, 0).astype(value.dtype)
    return lax.psum(kept, axis)


def update_slots(working, next_rows, column_factor, slot_low, slot_high):
    product = jnp.einsum(
        "atp,bsp->atbs",
        next_rows,
        column_factor,
        precision=HIGHEST,
        preferred_element_type=jnp.float32,
    )
    return working.at[:, :, slot_low:slot_high, :].add(-product)


def _chol_inverse_kernel(a_ref, l_ref, x_ref, lt_scr):
    size = a_ref.shape[0]
    block = a_ref[...]
    current = 0.5 * (block + block.T)
    lanes = lax.broadcasted_iota(jnp.int32, (size, size), 1)
    subs = lax.broadcasted_iota(jnp.int32, (size, size), 0)
    inverse = jnp.where(lanes == subs, 1.0, 0.0).astype(jnp.float32)
    lt_scr[...] = jnp.zeros((size, size), jnp.float32)
    row_ids = lax.broadcasted_iota(jnp.int32, (1, size), 1)
    group = 8
    for phase in range(size // group):
        top = phase * group
        active = size - top
        col_ids = lax.broadcasted_iota(jnp.int32, (active, 1), 0) + top
        for t in range(group):
            j = top + t
            row = current[t : t + 1, :]
            pivot = row[:, j : j + 1]
            root = jnp.sqrt(pivot)
            scale = lax.rsqrt(pivot)
            l_row = jnp.where(row_ids > j, row * scale, 0.0)
            l_row = jnp.where(row_ids == j, root, l_row)
            l_col = jnp.where(col_ids > j, current[:, j : j + 1] * scale, 0.0)
            l_col = jnp.where(col_ids == j, root, l_col)
            current = current - l_col * l_row
            lt_scr[j : j + 1, :] = l_row
            x_row = inverse[t : t + 1, :] * scale
            x_ref[j : j + 1, :] = x_row
            strict = jnp.where(col_ids > j, l_col, 0.0)
            inverse = inverse - strict * x_row
        current = current[group:, :]
        inverse = inverse[group:, :]
    l_ref[...] = lt_scr[...].T


def chol_inverse(block):
    size = block.shape[0]
    shape = jax.ShapeDtypeStruct((size, size), jnp.float32)
    return pl.pallas_call(
        _chol_inverse_kernel,
        out_shape=(shape, shape),
        scratch_shapes=[pltpu.VMEM((size, size), jnp.float32)],
    )(block)


def tall_cholesky(diagonal_block, below_rows):
    size = diagonal_block.shape[0]
    remaining = diagonal_block
    diag_columns = []
    inverses = []
    for step in range(size // TILE):
        low = step * TILE
        left = size - low - TILE
        pivot = remaining[:TILE, :TILE]
        pivot_factor, pivot_inverse = chol_inverse(pivot)
        inverses.append(pivot_inverse)
        parts = [jnp.zeros((low, TILE), jnp.float32), pivot_factor]
        if left:
            solved = jnp.dot(
                remaining[TILE:, :TILE],
                pivot_inverse.T,
                precision=HIGHEST,
                preferred_element_type=jnp.float32,
            )
            parts.append(solved)
            update = jnp.dot(
                solved, solved.T, precision=HIGHEST, preferred_element_type=jnp.float32
            )
            remaining = remaining[TILE:, TILE:] - update
        diag_columns.append(jnp.concatenate(parts, axis=0))
    lower_factor = jnp.concatenate(diag_columns, axis=1)
    rest = below_rows
    below_columns = []
    for step in range(size // TILE):
        low = step * TILE
        solved = jnp.dot(
            rest[:, :TILE], inverses[step].T, precision=HIGH, preferred_element_type=jnp.float32
        )
        below_columns.append(solved)
        if low + TILE < size:
            update = jnp.dot(
                solved,
                lower_factor[low + TILE :, low : low + TILE].T,
                precision=HIGH,
                preferred_element_type=jnp.float32,
            )
            rest = rest[:, TILE:] - update
    return lower_factor, jnp.concatenate(below_columns, axis=1)

def per_device(front, parent, tile_map, col_shift):
    leaf_count = lax.axis_size("leaf")
    row_count = lax.axis_size("row")
    col_count = lax.axis_size("col")
    leaf_index = lax.axis_index("leaf")
    row_index = lax.axis_index("row")
    col_index = lax.axis_index("col")
    local_front = front[0, :, 0, :, :, 0, :]
    row_slots = local_front.shape[0]
    col_slots = local_front.shape[2]
    pivot_tiles = NPIV // TILE
    assert pivot_tiles == row_count and pivot_tiles <= col_count
    row_tiles = jnp.arange(row_slots, dtype=jnp.int32) * row_count + row_index
    col_tiles = jnp.arange(col_slots, dtype=jnp.int32) * col_count + col_index

    working = local_front
    first_tiles = lax.all_gather(working[0, :, 0, :], "col", axis=0, tiled=False)
    diag_row = first_tiles[:pivot_tiles].transpose(1, 0, 2).reshape(TILE, NPIV)
    diagonal_block = lax.all_gather(diag_row, "row", axis=0, tiled=True)
    rest_cols, top_input, diagonal_block = lax.optimization_barrier(
        (working[1:, :, 0, :], working[0], diagonal_block)
    )
    first_cols = lax.all_gather(rest_cols, "col", axis=0, tiled=False)
    row_panel = first_cols[:pivot_tiles].transpose(1, 2, 0, 3).reshape(row_slots - 1, TILE, NPIV)
    top_rows = lax.all_gather(top_input, "row", axis=0, tiled=False)
    column_panel = top_rows.transpose(2, 3, 0, 1).reshape(col_slots, TILE, NPIV)
    stacked = jnp.concatenate(
        [row_panel.reshape(-1, NPIV), column_panel.reshape(-1, NPIV)], axis=0
    )
    lower_factor, solved = tall_cholesky(diagonal_block, stacked)
    trailing_rows = (row_slots - 1) * TILE
    row_factor = solved[:trailing_rows].reshape(row_slots - 1, TILE, NPIV)
    column_factor = solved[trailing_rows:].reshape(col_slots, TILE, NPIV)
    column_factor = jnp.where(
        (col_tiles >= pivot_tiles)[:, None, None], column_factor, 0.0
    )
    product = jnp.einsum(
        "atk,bsk->atbs",
        row_factor,
        column_factor,
        precision=HIGH,
        preferred_element_type=jnp.float32,
    )
    trailing = working[1:] - product
    own_col = jnp.minimum(col_index, pivot_tiles - 1)
    row_factor_cols = lax.dynamic_slice_in_dim(row_factor, own_col * TILE, TILE, 2)
    is_factor_col = (col_tiles < pivot_tiles)[None, None, :, None]
    trailing = jnp.where(is_factor_col, row_factor_cols[:, :, None, :], trailing)
    diag_rows = lax.dynamic_slice_in_dim(lower_factor, row_index * TILE, TILE, 0)
    diag_tile = lax.dynamic_slice_in_dim(diag_rows, own_col * TILE, TILE, 1)
    local_ids = jnp.arange(TILE, dtype=jnp.int32)
    global_row = row_index * TILE + local_ids[:, None]
    global_col = own_col * TILE + local_ids[None, :]
    diag_tile = jnp.where(global_row >= global_col, diag_tile, 0.0)
    top = jnp.where(is_factor_col[0], diag_tile[:, None, :], 0.0)
    top = jnp.broadcast_to(top, working[0].shape)
    working = jnp.concatenate([top[None], trailing], axis=0)
    factored = working.reshape(front.shape)
    contribution = jnp.where((col_tiles >= pivot_tiles)[None, None, :, None], working, 0.0)
    contrib_count = tile_map.shape[1]
    entry_ids = jnp.arange(contrib_count, dtype=jnp.int32)
    own_map = lax.dynamic_index_in_dim(tile_map, leaf_index, 0, keepdims=False)
    row_match = (row_tiles - pivot_tiles)[:, None] == entry_ids[None, :]
    row_targets = jnp.sum(jnp.where(row_match, own_map[None, :], 0), axis=1)
    row_valid = row_tiles >= pivot_tiles
    owner_count = leaf_count * row_count
    destination = row_targets % owner_count
    parent_row_slot = row_targets // owner_count
    slot_ids = jnp.arange(row_slots, dtype=jnp.int32)
    same_before = (
        (destination[None, :] == destination[:, None])
        & row_valid[None, :]
        & (slot_ids[None, :] < slot_ids[:, None])
    )
    rank_in_dest = jnp.sum(same_before.astype(jnp.int32), axis=1)
    capacity = (col_slots + row_count - 1) // row_count
    owner_ids = jnp.arange(owner_count, dtype=jnp.int32)
    capacity_ids = jnp.arange(capacity, dtype=jnp.int32)
    selection = (
        row_valid[None, None, :]
        & (destination[None, None, :] == owner_ids[:, None, None])
        & (rank_in_dest[None, None, :] == capacity_ids[None, :, None])
    )
    flattened = contribution.reshape(row_slots, -1)
    send_buffer = jnp.einsum(
        "oka,ax->okx",
        selection.astype(jnp.float32),
        flattened,
        precision=HIGHEST,
        preferred_element_type=jnp.float32,
    )
    received = lax.all_to_all(
        send_buffer, ("leaf", "row"), split_axis=0, concat_axis=0, tiled=True
    )
    received = received.reshape(leaf_count, row_count, capacity, -1)
    my_owner = leaf_index * row_count + row_index
    by_source = tile_map.reshape(leaf_count, contrib_count // row_count, row_count)
    source_hit = by_source % owner_count == my_owner
    received_slots = jnp.where(
        jnp.any(source_hit, axis=1),
        jnp.sum(jnp.where(source_hit, by_source // owner_count, 0), axis=1),
        -1,
    ).reshape(leaf_count, row_count, capacity)
    parent_local = parent[:, 0, 0, :, :, 0, :]
    parent_rows = parent_local.shape[0]
    parent_cols = parent_local.shape[2]
    row_place = (
        received_slots[None] == jnp.arange(parent_rows, dtype=jnp.int32)[:, None, None, None]
    ).astype(jnp.float32)
    by_leaf = jnp.einsum(
        "slrk,lrkx->slx", row_place, received, precision=HIGHEST, preferred_element_type=jnp.float32
    )
    by_leaf = by_leaf.reshape(parent_rows, leaf_count, TILE, col_slots, TILE)
    col_match = (col_tiles - pivot_tiles)[:, None] == entry_ids[None, :]
    col_targets = jnp.sum(jnp.where(col_match[None], tile_map[:, None, :], 0), axis=2)
    col_valid = col_tiles >= pivot_tiles
    parent_slot_ids = jnp.arange(parent_cols, dtype=jnp.int32)
    col_place = (
        col_valid[None, None, :]
        & (col_targets[:, None, :] // col_count == parent_slot_ids[None, :, None])
    ).astype(jnp.float32)
    assembled = jnp.einsum(
        "sltbv,lub->stuv", by_leaf, col_place, precision=HIGHEST, preferred_element_type=jnp.float32
    )
    new_parent = (parent_local + assembled).reshape(parent.shape)
    return (factored, new_parent)


def solution(mesh):
    return jax.shard_map(
        per_device,
        mesh=mesh,
        in_specs=(
            P("leaf", None, "row", None, None, "col", None),
            P(None, "leaf", "row", None, None, "col", None),
            P(),
            P(),
        ),
        out_specs=(
            P("leaf", None, "row", None, None, "col", None),
            P(None, "leaf", "row", None, None, "col", None),
        ),
        check_vma=False,
    )
```

```python
import jax
import jax.numpy as jnp
from jax import lax
from jax.sharding import PartitionSpec as P
from jax.experimental import pallas as pl
from jax.experimental.pallas import tpu as pltpu

TILE = 128
PB = 512
PANELS = 2
NPIV = 1024


HIGHEST = lax.Precision.HIGHEST
HIGH = lax.Precision.HIGH


def spread(value, axis, source):
    kept = jnp.where(lax.axis_index(axis) == source, value, 0).astype(value.dtype)
    return lax.psum(kept, axis)


def update_slots(working, next_rows, column_factor, slot_low, slot_high):
    product = jnp.einsum(
        "atp,bsp->atbs",
        next_rows,
        column_factor,
        precision=HIGHEST,
        preferred_element_type=jnp.float32,
    )
    return working.at[:, :, slot_low:slot_high, :].add(-product)


def _chol_inverse_kernel(a_ref, l_ref, x_ref, lt_scr):
    size = a_ref.shape[0]
    block = a_ref[...]
    current = 0.5 * (block + block.T)
    lanes = lax.broadcasted_iota(jnp.int32, (size, size), 1)
    subs = lax.broadcasted_iota(jnp.int32, (size, size), 0)
    inverse = jnp.where(lanes == subs, 1.0, 0.0).astype(jnp.float32)
    lt_scr[...] = jnp.zeros((size, size), jnp.float32)
    row_ids = lax.broadcasted_iota(jnp.int32, (1, size), 1)
    group = 8
    for phase in range(size // group):
        top = phase * group
        active = size - top
        col_ids = lax.broadcasted_iota(jnp.int32, (active, 1), 0) + top
        for t in range(group):
            j = top + t
            row = current[t : t + 1, :]
            pivot = row[:, j : j + 1]
            root = jnp.sqrt(pivot)
            scale = lax.rsqrt(pivot)
            l_row = jnp.where(row_ids > j, row * scale, 0.0)
            l_row = jnp.where(row_ids == j, root, l_row)
            l_col = jnp.where(col_ids > j, current[:, j : j + 1] * scale, 0.0)
            l_col = jnp.where(col_ids == j, root, l_col)
            current = current - l_col * l_row
            lt_scr[j : j + 1, :] = l_row
            x_row = inverse[t : t + 1, :] * scale
            x_ref[j : j + 1, :] = x_row
            strict = jnp.where(col_ids > j, l_col, 0.0)
            inverse = inverse - strict * x_row
        current = current[group:, :]
        inverse = inverse[group:, :]
    l_ref[...] = lt_scr[...].T


def chol_inverse(block):
    size = block.shape[0]
    shape = jax.ShapeDtypeStruct((size, size), jnp.float32)
    return pl.pallas_call(
        _chol_inverse_kernel,
        out_shape=(shape, shape),
        scratch_shapes=[pltpu.VMEM((size, size), jnp.float32)],
    )(block)


def tall_cholesky(diagonal_block, below_rows):
    size = diagonal_block.shape[0]
    remaining = diagonal_block
    diag_columns = []
    inverses = []
    for step in range(size // TILE):
        low = step * TILE
        left = size - low - TILE
        pivot = remaining[:TILE, :TILE]
        pivot_factor, pivot_inverse = chol_inverse(pivot)
        inverses.append(pivot_inverse)
        parts = [jnp.zeros((low, TILE), jnp.float32), pivot_factor]
        if left:
            solved = jnp.dot(
                remaining[TILE:, :TILE],
                pivot_inverse.T,
                precision=HIGHEST,
                preferred_element_type=jnp.float32,
            )
            parts.append(solved)
            update = jnp.dot(
                solved, solved.T, precision=HIGHEST, preferred_element_type=jnp.float32
            )
            remaining = remaining[TILE:, TILE:] - update
        diag_columns.append(jnp.concatenate(parts, axis=0))
    lower_factor = jnp.concatenate(diag_columns, axis=1)
    rest = below_rows
    below_columns = []
    for step in range(size // TILE):
        low = step * TILE
        solved = jnp.dot(
            rest[:, :TILE], inverses[step].T, precision=HIGH, preferred_element_type=jnp.float32
        )
        below_columns.append(solved)
        if low + TILE < size:
            update = jnp.dot(
                solved,
                lower_factor[low + TILE :, low : low + TILE].T,
                precision=HIGH,
                preferred_element_type=jnp.float32,
            )
            rest = rest[:, TILE:] - update
    return lower_factor, jnp.concatenate(below_columns, axis=1)

def per_device(front, parent, tile_map, col_shift):
    leaf_count = lax.axis_size("leaf")
    row_count = lax.axis_size("row")
    col_count = lax.axis_size("col")
    leaf_index = lax.axis_index("leaf")
    row_index = lax.axis_index("row")
    col_index = lax.axis_index("col")
    local_front = front[0, :, 0, :, :, 0, :]
    row_slots = local_front.shape[0]
    col_slots = local_front.shape[2]
    pivot_tiles = NPIV // TILE
    assert pivot_tiles == row_count and pivot_tiles <= col_count
    row_tiles = jnp.arange(row_slots, dtype=jnp.int32) * row_count + row_index
    col_tiles = jnp.arange(col_slots, dtype=jnp.int32) * col_count + col_index

    working = local_front
    first_tiles = lax.all_gather(working[0, :, 0, :], "col", axis=0, tiled=False)
    diag_row = first_tiles[:pivot_tiles].transpose(1, 0, 2).reshape(TILE, NPIV)
    diagonal_block = lax.all_gather(diag_row, "row", axis=0, tiled=True)
    rest_cols, top_input, diagonal_block = lax.optimization_barrier(
        (working[1:, :, 0, :], working[0], diagonal_block)
    )
    first_cols = lax.all_gather(rest_cols, "col", axis=0, tiled=False)
    row_panel = first_cols[:pivot_tiles].transpose(1, 2, 0, 3).reshape(row_slots - 1, TILE, NPIV)
    top_rows = lax.all_gather(top_input, "row", axis=0, tiled=False)
    column_panel = top_rows.transpose(2, 3, 0, 1).reshape(col_slots, TILE, NPIV)
    stacked = jnp.concatenate(
        [row_panel.reshape(-1, NPIV), column_panel.reshape(-1, NPIV)], axis=0
    )
    lower_factor, solved = tall_cholesky(diagonal_block, stacked)
    trailing_rows = (row_slots - 1) * TILE
    row_factor = solved[:trailing_rows].reshape(row_slots - 1, TILE, NPIV)
    column_factor = solved[trailing_rows:].reshape(col_slots, TILE, NPIV)
    column_factor = jnp.where(
        (col_tiles >= pivot_tiles)[:, None, None], column_factor, 0.0
    )
    product = jnp.einsum(
        "atk,bsk->atbs",
        row_factor,
        column_factor,
        precision=HIGH,
        preferred_element_type=jnp.float32,
    )
    trailing = working[1:] - product
    own_col = jnp.minimum(col_index, pivot_tiles - 1)
    row_factor_cols = lax.dynamic_slice_in_dim(row_factor, own_col * TILE, TILE, 2)
    is_factor_col = (col_tiles < pivot_tiles)[None, None, :, None]
    trailing = jnp.where(is_factor_col, row_factor_cols[:, :, None, :], trailing)
    diag_rows = lax.dynamic_slice_in_dim(lower_factor, row_index * TILE, TILE, 0)
    diag_tile = lax.dynamic_slice_in_dim(diag_rows, own_col * TILE, TILE, 1)
    local_ids = jnp.arange(TILE, dtype=jnp.int32)
    global_row = row_index * TILE + local_ids[:, None]
    global_col = own_col * TILE + local_ids[None, :]
    diag_tile = jnp.where(global_row >= global_col, diag_tile, 0.0)
    top = jnp.where(is_factor_col[0], diag_tile[:, None, :], 0.0)
    top = jnp.broadcast_to(top, working[0].shape)
    working = jnp.concatenate([top[None], trailing], axis=0)
    factored = working.reshape(front.shape)
    contribution = jnp.where((col_tiles >= pivot_tiles)[None, None, :, None], working, 0.0)
    contrib_count = tile_map.shape[1]
    entry_ids = jnp.arange(contrib_count, dtype=jnp.int32)
    own_map = lax.dynamic_index_in_dim(tile_map, leaf_index, 0, keepdims=False)
    row_match = (row_tiles - pivot_tiles)[:, None] == entry_ids[None, :]
    row_targets = jnp.sum(jnp.where(row_match, own_map[None, :], 0), axis=1)
    row_valid = row_tiles >= pivot_tiles
    owner_count = leaf_count * row_count
    destination = row_targets % owner_count
    parent_row_slot = row_targets // owner_count
    slot_ids = jnp.arange(row_slots, dtype=jnp.int32)
    same_before = (
        (destination[None, :] == destination[:, None])
        & row_valid[None, :]
        & (slot_ids[None, :] < slot_ids[:, None])
    )
    rank_in_dest = jnp.sum(same_before.astype(jnp.int32), axis=1)
    capacity = (col_slots + row_count - 1) // row_count
    owner_ids = jnp.arange(owner_count, dtype=jnp.int32)
    capacity_ids = jnp.arange(capacity, dtype=jnp.int32)
    selection = (
        row_valid[None, None, :]
        & (destination[None, None, :] == owner_ids[:, None, None])
        & (rank_in_dest[None, None, :] == capacity_ids[None, :, None])
    )
    flattened = contribution.reshape(row_slots, -1, TILE)
    send_buffer = jnp.einsum(
        "oka,axy->okxy",
        selection.astype(jnp.float32),
        flattened,
        precision=HIGHEST,
        preferred_element_type=jnp.float32,
    )
    send_buffer = send_buffer.reshape(owner_count * capacity, -1, TILE)
    received = lax.all_to_all(
        send_buffer, ("leaf", "row"), split_axis=0, concat_axis=0, tiled=True
    )
    received = received.reshape(leaf_count, row_count, capacity, -1, TILE)
    my_owner = leaf_index * row_count + row_index
    by_source = tile_map.reshape(leaf_count, contrib_count // row_count, row_count)
    source_hit = by_source % owner_count == my_owner
    received_slots = jnp.where(
        jnp.any(source_hit, axis=1),
        jnp.sum(jnp.where(source_hit, by_source // owner_count, 0), axis=1),
        -1,
    ).reshape(leaf_count, row_count, capacity)
    parent_local = parent[:, 0, 0, :, :, 0, :]
    parent_rows = parent_local.shape[0]
    parent_cols = parent_local.shape[2]
    row_place = (
        received_slots[None] == jnp.arange(parent_rows, dtype=jnp.int32)[:, None, None, None]
    ).astype(jnp.float32)
    by_leaf = jnp.einsum(
        "slrk,lrkxy->slxy", row_place, received, precision=HIGHEST, preferred_element_type=jnp.float32
    )
    by_leaf = by_leaf.reshape(parent_rows, leaf_count, TILE, col_slots, TILE)
    col_match = (col_tiles - pivot_tiles)[:, None] == entry_ids[None, :]
    col_targets = jnp.sum(jnp.where(col_match[None], tile_map[:, None, :], 0), axis=2)
    col_valid = col_tiles >= pivot_tiles
    parent_slot_ids = jnp.arange(parent_cols, dtype=jnp.int32)
    col_place = (
        col_valid[None, None, :]
        & (col_targets[:, None, :] // col_count == parent_slot_ids[None, :, None])
    ).astype(jnp.float32)
    assembled = jnp.einsum(
        "sltbv,lub->stuv", by_leaf, col_place, precision=HIGHEST, preferred_element_type=jnp.float32
    )
    new_parent = (parent_local + assembled).reshape(parent.shape)
    return (factored, new_parent)


def solution(mesh):
    return jax.shard_map(
        per_device,
        mesh=mesh,
        in_specs=(
            P("leaf", None, "row", None, None, "col", None),
            P(None, "leaf", "row", None, None, "col", None),
            P(),
            P(),
        ),
        out_specs=(
            P("leaf", None, "row", None, None, "col", None),
            P(None, "leaf", "row", None, None, "col", None),
        ),
        check_vma=False,
    )
```

```python
import jax
import jax.numpy as jnp
from jax import lax
from jax.sharding import PartitionSpec as P
from jax.experimental import pallas as pl
from jax.experimental.pallas import tpu as pltpu

TILE = 128
PB = 512
PANELS = 2
NPIV = 1024


HIGHEST = lax.Precision.HIGHEST
HIGH = lax.Precision.HIGH


def spread(value, axis, source):
    kept = jnp.where(lax.axis_index(axis) == source, value, 0).astype(value.dtype)
    return lax.psum(kept, axis)


def update_slots(working, next_rows, column_factor, slot_low, slot_high):
    product = jnp.einsum(
        "atp,bsp->atbs",
        next_rows,
        column_factor,
        precision=HIGHEST,
        preferred_element_type=jnp.float32,
    )
    return working.at[:, :, slot_low:slot_high, :].add(-product)


def _chol_inverse_kernel(a_ref, l_ref, x_ref, lt_scr):
    size = a_ref.shape[0]
    block = a_ref[...]
    current = 0.5 * (block + block.T)
    lanes = lax.broadcasted_iota(jnp.int32, (size, size), 1)
    subs = lax.broadcasted_iota(jnp.int32, (size, size), 0)
    inverse = jnp.where(lanes == subs, 1.0, 0.0).astype(jnp.float32)
    lt_scr[...] = jnp.zeros((size, size), jnp.float32)
    row_ids = lax.broadcasted_iota(jnp.int32, (1, size), 1)
    group = 8
    for phase in range(size // group):
        top = phase * group
        active = size - top
        col_ids = lax.broadcasted_iota(jnp.int32, (active, 1), 0) + top
        for t in range(group):
            j = top + t
            row = current[t : t + 1, :]
            pivot = row[:, j : j + 1]
            root = jnp.sqrt(pivot)
            scale = lax.rsqrt(pivot)
            l_row = jnp.where(row_ids > j, row * scale, 0.0)
            l_row = jnp.where(row_ids == j, root, l_row)
            l_col = jnp.where(col_ids > j, current[:, j : j + 1] * scale, 0.0)
            l_col = jnp.where(col_ids == j, root, l_col)
            current = current - l_col * l_row
            lt_scr[j : j + 1, :] = l_row
            x_row = inverse[t : t + 1, :] * scale
            x_ref[j : j + 1, :] = x_row
            strict = jnp.where(col_ids > j, l_col, 0.0)
            inverse = inverse - strict * x_row
        current = current[group:, :]
        inverse = inverse[group:, :]
    l_ref[...] = lt_scr[...].T


def chol_inverse(block):
    size = block.shape[0]
    shape = jax.ShapeDtypeStruct((size, size), jnp.float32)
    return pl.pallas_call(
        _chol_inverse_kernel,
        out_shape=(shape, shape),
        scratch_shapes=[pltpu.VMEM((size, size), jnp.float32)],
    )(block)


def tall_cholesky(diagonal_block, below_rows):
    size = diagonal_block.shape[0]
    remaining = diagonal_block
    diag_columns = []
    inverses = []
    for step in range(size // TILE):
        low = step * TILE
        left = size - low - TILE
        pivot = remaining[:TILE, :TILE]
        pivot_factor, pivot_inverse = chol_inverse(pivot)
        inverses.append(pivot_inverse)
        parts = [jnp.zeros((low, TILE), jnp.float32), pivot_factor]
        if left:
            solved = jnp.dot(
                remaining[TILE:, :TILE],
                pivot_inverse.T,
                precision=HIGH,
                preferred_element_type=jnp.float32,
            )
            parts.append(solved)
            update = jnp.dot(
                solved, solved.T, precision=HIGH, preferred_element_type=jnp.float32
            )
            remaining = remaining[TILE:, TILE:] - update
        diag_columns.append(jnp.concatenate(parts, axis=0))
    lower_factor = jnp.concatenate(diag_columns, axis=1)
    rest = below_rows
    below_columns = []
    for step in range(size // TILE):
        low = step * TILE
        solved = jnp.dot(
            rest[:, :TILE], inverses[step].T, precision=HIGH, preferred_element_type=jnp.float32
        )
        below_columns.append(solved)
        if low + TILE < size:
            update = jnp.dot(
                solved,
                lower_factor[low + TILE :, low : low + TILE].T,
                precision=HIGH,
                preferred_element_type=jnp.float32,
            )
            rest = rest[:, TILE:] - update
    return lower_factor, jnp.concatenate(below_columns, axis=1)

def per_device(front, parent, tile_map, col_shift):
    leaf_count = lax.axis_size("leaf")
    row_count = lax.axis_size("row")
    col_count = lax.axis_size("col")
    leaf_index = lax.axis_index("leaf")
    row_index = lax.axis_index("row")
    col_index = lax.axis_index("col")
    local_front = front[0, :, 0, :, :, 0, :]
    row_slots = local_front.shape[0]
    col_slots = local_front.shape[2]
    pivot_tiles = NPIV // TILE
    assert pivot_tiles == row_count and pivot_tiles <= col_count
    row_tiles = jnp.arange(row_slots, dtype=jnp.int32) * row_count + row_index
    col_tiles = jnp.arange(col_slots, dtype=jnp.int32) * col_count + col_index

    working = local_front
    first_tiles = lax.all_gather(working[0, :, 0, :], "col", axis=0, tiled=False)
    diag_row = first_tiles[:pivot_tiles].transpose(1, 0, 2).reshape(TILE, NPIV)
    diagonal_block = lax.all_gather(diag_row, "row", axis=0, tiled=True)
    rest_cols, top_input, diagonal_block = lax.optimization_barrier(
        (working[1:, :, 0, :], working[0], diagonal_block)
    )
    first_cols = lax.all_gather(rest_cols, "col", axis=0, tiled=False)
    row_panel = first_cols[:pivot_tiles].transpose(1, 2, 0, 3).reshape(row_slots - 1, TILE, NPIV)
    top_rows = lax.all_gather(top_input, "row", axis=0, tiled=False)
    column_panel = top_rows.transpose(2, 3, 0, 1).reshape(col_slots, TILE, NPIV)
    stacked = jnp.concatenate(
        [row_panel.reshape(-1, NPIV), column_panel.reshape(-1, NPIV)], axis=0
    )
    lower_factor, solved = tall_cholesky(diagonal_block, stacked)
    trailing_rows = (row_slots - 1) * TILE
    row_factor = solved[:trailing_rows].reshape(row_slots - 1, TILE, NPIV)
    column_factor = solved[trailing_rows:].reshape(col_slots, TILE, NPIV)
    column_factor = jnp.where(
        (col_tiles >= pivot_tiles)[:, None, None], column_factor, 0.0
    )
    product = jnp.einsum(
        "atk,bsk->atbs",
        row_factor,
        column_factor,
        precision=HIGH,
        preferred_element_type=jnp.float32,
    )
    trailing = working[1:] - product
    own_col = jnp.minimum(col_index, pivot_tiles - 1)
    row_factor_cols = lax.dynamic_slice_in_dim(row_factor, own_col * TILE, TILE, 2)
    is_factor_col = (col_tiles < pivot_tiles)[None, None, :, None]
    trailing = jnp.where(is_factor_col, row_factor_cols[:, :, None, :], trailing)
    diag_rows = lax.dynamic_slice_in_dim(lower_factor, row_index * TILE, TILE, 0)
    diag_tile = lax.dynamic_slice_in_dim(diag_rows, own_col * TILE, TILE, 1)
    local_ids = jnp.arange(TILE, dtype=jnp.int32)
    global_row = row_index * TILE + local_ids[:, None]
    global_col = own_col * TILE + local_ids[None, :]
    diag_tile = jnp.where(global_row >= global_col, diag_tile, 0.0)
    top = jnp.where(is_factor_col[0], diag_tile[:, None, :], 0.0)
    top = jnp.broadcast_to(top, working[0].shape)
    working = jnp.concatenate([top[None], trailing], axis=0)
    factored = working.reshape(front.shape)
    contribution = jnp.where((col_tiles >= pivot_tiles)[None, None, :, None], working, 0.0)
    contrib_count = tile_map.shape[1]
    entry_ids = jnp.arange(contrib_count, dtype=jnp.int32)
    own_map = lax.dynamic_index_in_dim(tile_map, leaf_index, 0, keepdims=False)
    row_match = (row_tiles - pivot_tiles)[:, None] == entry_ids[None, :]
    row_targets = jnp.sum(jnp.where(row_match, own_map[None, :], 0), axis=1)
    row_valid = row_tiles >= pivot_tiles
    owner_count = leaf_count * row_count
    destination = row_targets % owner_count
    parent_row_slot = row_targets // owner_count
    slot_ids = jnp.arange(row_slots, dtype=jnp.int32)
    same_before = (
        (destination[None, :] == destination[:, None])
        & row_valid[None, :]
        & (slot_ids[None, :] < slot_ids[:, None])
    )
    rank_in_dest = jnp.sum(same_before.astype(jnp.int32), axis=1)
    capacity = (col_slots + row_count - 1) // row_count
    owner_ids = jnp.arange(owner_count, dtype=jnp.int32)
    capacity_ids = jnp.arange(capacity, dtype=jnp.int32)
    selection = (
        row_valid[None, None, :]
        & (destination[None, None, :] == owner_ids[:, None, None])
        & (rank_in_dest[None, None, :] == capacity_ids[None, :, None])
    )
    flattened = contribution.reshape(row_slots, -1, TILE)
    send_buffer = jnp.einsum(
        "oka,axy->okxy",
        selection.astype(jnp.float32),
        flattened,
        precision=HIGHEST,
        preferred_element_type=jnp.float32,
    )
    send_buffer = send_buffer.reshape(owner_count * capacity, -1, TILE)
    received = lax.all_to_all(
        send_buffer, ("leaf", "row"), split_axis=0, concat_axis=0, tiled=True
    )
    received = received.reshape(leaf_count, row_count, capacity, -1, TILE)
    my_owner = leaf_index * row_count + row_index
    by_source = tile_map.reshape(leaf_count, contrib_count // row_count, row_count)
    source_hit = by_source % owner_count == my_owner
    received_slots = jnp.where(
        jnp.any(source_hit, axis=1),
        jnp.sum(jnp.where(source_hit, by_source // owner_count, 0), axis=1),
        -1,
    ).reshape(leaf_count, row_count, capacity)
    parent_local = parent[:, 0, 0, :, :, 0, :]
    parent_rows = parent_local.shape[0]
    parent_cols = parent_local.shape[2]
    row_place = (
        received_slots[None] == jnp.arange(parent_rows, dtype=jnp.int32)[:, None, None, None]
    ).astype(jnp.float32)
    by_leaf = jnp.einsum(
        "slrk,lrkxy->slxy", row_place, received, precision=HIGHEST, preferred_element_type=jnp.float32
    )
    by_leaf = by_leaf.reshape(parent_rows, leaf_count, TILE, col_slots, TILE)
    col_match = (col_tiles - pivot_tiles)[:, None] == entry_ids[None, :]
    col_targets = jnp.sum(jnp.where(col_match[None], tile_map[:, None, :], 0), axis=2)
    col_valid = col_tiles >= pivot_tiles
    parent_slot_ids = jnp.arange(parent_cols, dtype=jnp.int32)
    col_place = (
        col_valid[None, None, :]
        & (col_targets[:, None, :] // col_count == parent_slot_ids[None, :, None])
    ).astype(jnp.float32)
    assembled = jnp.einsum(
        "sltbv,lub->stuv", by_leaf, col_place, precision=HIGHEST, preferred_element_type=jnp.float32
    )
    new_parent = (parent_local + assembled).reshape(parent.shape)
    return (factored, new_parent)


def solution(mesh):
    return jax.shard_map(
        per_device,
        mesh=mesh,
        in_specs=(
            P("leaf", None, "row", None, None, "col", None),
            P(None, "leaf", "row", None, None, "col", None),
            P(),
            P(),
        ),
        out_specs=(
            P("leaf", None, "row", None, None, "col", None),
            P(None, "leaf", "row", None, None, "col", None),
        ),
        check_vma=False,
    )
```

```python
import jax
import jax.numpy as jnp
from jax import lax
from jax.sharding import PartitionSpec as P
from jax.experimental import pallas as pl
from jax.experimental.pallas import tpu as pltpu

TILE = 128
PB = 512
PANELS = 2
NPIV = 1024


HIGHEST = lax.Precision.HIGHEST
HIGH = lax.Precision.HIGH


def spread(value, axis, source):
    kept = jnp.where(lax.axis_index(axis) == source, value, 0).astype(value.dtype)
    return lax.psum(kept, axis)


def update_slots(working, next_rows, column_factor, slot_low, slot_high):
    product = jnp.einsum(
        "atp,bsp->atbs",
        next_rows,
        column_factor,
        precision=HIGHEST,
        preferred_element_type=jnp.float32,
    )
    return working.at[:, :, slot_low:slot_high, :].add(-product)


def _chol_inverse_kernel(a_ref, l_ref, x_ref, lt_scr):
    size = a_ref.shape[0]
    current = a_ref[...]
    lanes = lax.broadcasted_iota(jnp.int32, (size, size), 1)
    subs = lax.broadcasted_iota(jnp.int32, (size, size), 0)
    inverse = jnp.where(lanes == subs, 1.0, 0.0).astype(jnp.float32)
    lt_scr[...] = jnp.zeros((size, size), jnp.float32)
    row_ids = lax.broadcasted_iota(jnp.int32, (1, size), 1)
    group = 8
    for phase in range(size // group):
        top = phase * group
        active = size - top
        col_ids = lax.broadcasted_iota(jnp.int32, (active, 1), 0) + top
        for t in range(group):
            j = top + t
            row = current[t : t + 1, :]
            pivot = row[:, j : j + 1]
            root = jnp.sqrt(pivot)
            scale = lax.rsqrt(pivot)
            l_row = jnp.where(row_ids > j, row * scale, 0.0)
            l_row = jnp.where(row_ids == j, root, l_row)
            l_col = jnp.where(col_ids > j, current[:, j : j + 1] * scale, 0.0)
            l_col = jnp.where(col_ids == j, root, l_col)
            current = current - l_col * l_row
            lt_scr[j : j + 1, :] = l_row
            x_row = inverse[t : t + 1, :] * scale
            x_ref[j : j + 1, :] = x_row
            strict = jnp.where(col_ids > j, l_col, 0.0)
            inverse = inverse - strict * x_row
        current = current[group:, :]
        inverse = inverse[group:, :]
    l_ref[...] = lt_scr[...].T


def chol_inverse(block):
    size = block.shape[0]
    shape = jax.ShapeDtypeStruct((size, size), jnp.float32)
    return pl.pallas_call(
        _chol_inverse_kernel,
        out_shape=(shape, shape),
        scratch_shapes=[pltpu.VMEM((size, size), jnp.float32)],
    )(block)


def tall_cholesky(diagonal_block, below_rows):
    size = diagonal_block.shape[0]
    remaining = diagonal_block
    diag_columns = []
    inverses = []
    for step in range(size // TILE):
        low = step * TILE
        left = size - low - TILE
        pivot = remaining[:TILE, :TILE]
        pivot_factor, pivot_inverse = chol_inverse(pivot)
        inverses.append(pivot_inverse)
        parts = [jnp.zeros((low, TILE), jnp.float32), pivot_factor]
        if left:
            solved = jnp.dot(
                remaining[TILE:, :TILE],
                pivot_inverse.T,
                precision=HIGH,
                preferred_element_type=jnp.float32,
            )
            parts.append(solved)
            update = jnp.dot(
                solved, solved.T, precision=HIGH, preferred_element_type=jnp.float32
            )
            remaining = remaining[TILE:, TILE:] - update
        diag_columns.append(jnp.concatenate(parts, axis=0))
    lower_factor = jnp.concatenate(diag_columns, axis=1)
    rest = below_rows
    below_columns = []
    for step in range(size // TILE):
        low = step * TILE
        solved = jnp.dot(
            rest[:, :TILE], inverses[step].T, precision=HIGH, preferred_element_type=jnp.float32
        )
        below_columns.append(solved)
        if low + TILE < size:
            update = jnp.dot(
                solved,
                lower_factor[low + TILE :, low : low + TILE].T,
                precision=HIGH,
                preferred_element_type=jnp.float32,
            )
            rest = rest[:, TILE:] - update
    return lower_factor, jnp.concatenate(below_columns, axis=1)

def per_device(front, parent, tile_map, col_shift):
    leaf_count = lax.axis_size("leaf")
    row_count = lax.axis_size("row")
    col_count = lax.axis_size("col")
    leaf_index = lax.axis_index("leaf")
    row_index = lax.axis_index("row")
    col_index = lax.axis_index("col")
    local_front = front[0, :, 0, :, :, 0, :]
    row_slots = local_front.shape[0]
    col_slots = local_front.shape[2]
    pivot_tiles = NPIV // TILE
    assert pivot_tiles == row_count and pivot_tiles <= col_count
    row_tiles = jnp.arange(row_slots, dtype=jnp.int32) * row_count + row_index
    col_tiles = jnp.arange(col_slots, dtype=jnp.int32) * col_count + col_index

    working = local_front
    first_tiles = lax.all_gather(working[0, :, 0, :], "col", axis=0, tiled=False)
    diag_row = first_tiles[:pivot_tiles].transpose(1, 0, 2).reshape(TILE, NPIV)
    diagonal_block = lax.all_gather(diag_row, "row", axis=0, tiled=True)
    rest_cols, top_input, diagonal_block = lax.optimization_barrier(
        (working[1:, :, 0, :], working[0], diagonal_block)
    )
    first_cols = lax.all_gather(rest_cols, "col", axis=0, tiled=False)
    row_panel = first_cols[:pivot_tiles].transpose(1, 2, 0, 3).reshape(row_slots - 1, TILE, NPIV)
    top_rows = lax.all_gather(top_input, "row", axis=0, tiled=False)
    column_panel = top_rows.transpose(2, 3, 0, 1).reshape(col_slots, TILE, NPIV)
    stacked = jnp.concatenate(
        [row_panel.reshape(-1, NPIV), column_panel.reshape(-1, NPIV)], axis=0
    )
    lower_factor, solved = tall_cholesky(diagonal_block, stacked)
    trailing_rows = (row_slots - 1) * TILE
    row_factor = solved[:trailing_rows].reshape(row_slots - 1, TILE, NPIV)
    column_factor = solved[trailing_rows:].reshape(col_slots, TILE, NPIV)
    column_factor = jnp.where(
        (col_tiles >= pivot_tiles)[:, None, None], column_factor, 0.0
    )
    product = jnp.einsum(
        "atk,bsk->atbs",
        row_factor,
        column_factor,
        precision=HIGH,
        preferred_element_type=jnp.float32,
    )
    trailing = working[1:] - product
    own_col = jnp.minimum(col_index, pivot_tiles - 1)
    row_factor_cols = lax.dynamic_slice_in_dim(row_factor, own_col * TILE, TILE, 2)
    is_factor_col = (col_tiles < pivot_tiles)[None, None, :, None]
    trailing = jnp.where(is_factor_col, row_factor_cols[:, :, None, :], trailing)
    diag_rows = lax.dynamic_slice_in_dim(lower_factor, row_index * TILE, TILE, 0)
    diag_tile = lax.dynamic_slice_in_dim(diag_rows, own_col * TILE, TILE, 1)
    local_ids = jnp.arange(TILE, dtype=jnp.int32)
    global_row = row_index * TILE + local_ids[:, None]
    global_col = own_col * TILE + local_ids[None, :]
    diag_tile = jnp.where(global_row >= global_col, diag_tile, 0.0)
    top = jnp.where(is_factor_col[0], diag_tile[:, None, :], 0.0)
    top = jnp.broadcast_to(top, working[0].shape)
    working = jnp.concatenate([top[None], trailing], axis=0)
    factored = working.reshape(front.shape)
    contribution = jnp.where((col_tiles >= pivot_tiles)[None, None, :, None], working, 0.0)
    contrib_count = tile_map.shape[1]
    entry_ids = jnp.arange(contrib_count, dtype=jnp.int32)
    own_map = lax.dynamic_index_in_dim(tile_map, leaf_index, 0, keepdims=False)
    row_match = (row_tiles - pivot_tiles)[:, None] == entry_ids[None, :]
    row_targets = jnp.sum(jnp.where(row_match, own_map[None, :], 0), axis=1)
    row_valid = row_tiles >= pivot_tiles
    owner_count = leaf_count * row_count
    destination = row_targets % owner_count
    parent_row_slot = row_targets // owner_count
    slot_ids = jnp.arange(row_slots, dtype=jnp.int32)
    same_before = (
        (destination[None, :] == destination[:, None])
        & row_valid[None, :]
        & (slot_ids[None, :] < slot_ids[:, None])
    )
    rank_in_dest = jnp.sum(same_before.astype(jnp.int32), axis=1)
    capacity = (col_slots + row_count - 1) // row_count
    owner_ids = jnp.arange(owner_count, dtype=jnp.int32)
    capacity_ids = jnp.arange(capacity, dtype=jnp.int32)
    selection = (
        row_valid[None, None, :]
        & (destination[None, None, :] == owner_ids[:, None, None])
        & (rank_in_dest[None, None, :] == capacity_ids[None, :, None])
    )
    flattened = contribution.reshape(row_slots, -1, TILE)
    send_buffer = jnp.einsum(
        "oka,axy->okxy",
        selection.astype(jnp.float32),
        flattened,
        precision=HIGHEST,
        preferred_element_type=jnp.float32,
    )
    send_buffer = send_buffer.reshape(owner_count * capacity, -1, TILE)
    received = lax.all_to_all(
        send_buffer, ("leaf", "row"), split_axis=0, concat_axis=0, tiled=True
    )
    received = received.reshape(leaf_count, row_count, capacity, -1, TILE)
    my_owner = leaf_index * row_count + row_index
    by_source = tile_map.reshape(leaf_count, contrib_count // row_count, row_count)
    source_hit = by_source % owner_count == my_owner
    received_slots = jnp.where(
        jnp.any(source_hit, axis=1),
        jnp.sum(jnp.where(source_hit, by_source // owner_count, 0), axis=1),
        -1,
    ).reshape(leaf_count, row_count, capacity)
    parent_local = parent[:, 0, 0, :, :, 0, :]
    parent_rows = parent_local.shape[0]
    parent_cols = parent_local.shape[2]
    row_place = (
        received_slots[None] == jnp.arange(parent_rows, dtype=jnp.int32)[:, None, None, None]
    ).astype(jnp.float32)
    by_leaf = jnp.einsum(
        "slrk,lrkxy->slxy", row_place, received, precision=HIGHEST, preferred_element_type=jnp.float32
    )
    by_leaf = by_leaf.reshape(parent_rows, leaf_count, TILE, col_slots, TILE)
    col_match = (col_tiles - pivot_tiles)[:, None] == entry_ids[None, :]
    col_targets = jnp.sum(jnp.where(col_match[None], tile_map[:, None, :], 0), axis=2)
    col_valid = col_tiles >= pivot_tiles
    parent_slot_ids = jnp.arange(parent_cols, dtype=jnp.int32)
    col_place = (
        col_valid[None, None, :]
        & (col_targets[:, None, :] // col_count == parent_slot_ids[None, :, None])
    ).astype(jnp.float32)
    assembled = jnp.einsum(
        "sltbv,lub->stuv", by_leaf, col_place, precision=HIGHEST, preferred_element_type=jnp.float32
    )
    new_parent = (parent_local + assembled).reshape(parent.shape)
    return (factored, new_parent)


def solution(mesh):
    return jax.shard_map(
        per_device,
        mesh=mesh,
        in_specs=(
            P("leaf", None, "row", None, None, "col", None),
            P(None, "leaf", "row", None, None, "col", None),
            P(),
            P(),
        ),
        out_specs=(
            P("leaf", None, "row", None, None, "col", None),
            P(None, "leaf", "row", None, None, "col", None),
        ),
        check_vma=False,
    )
```
